256 devices in a mesh: kv: 8 (over y, core), blk: 32 (over x, z).
Axes of the slice: x: 4, y: 4, z: 8, core: 2. Of those that a mesh axis runs over, the one named last changes fastest.
Arguments:
- queries: bfloat16 [256, 8192], P('blk', 'kv'), may hold values from -40 to 40
- draft_token_keys: bfloat16 [256, 1024], P('blk', 'kv'), may hold values from -15 to 15
- draft_token_values: bfloat16 [256, 1024], P('blk', 'kv'), may hold values from -6 to 6
- cached_key_vectors: bfloat16 [4, 4096, 1024], P(None, 'blk', 'kv'), may hold values from -40 to 40
- cached_value_vectors: bfloat16 [4, 4096, 1024], P(None, 'blk', 'kv'), may hold values from -6 to 6
- out_weight: bfloat16 [8192, 8192], P('kv', 'blk'), may hold values from -0.5 to 0.5
- lengths: int32 [4], replicated, may hold values from 256 to 4088, as said below
- parents: int32 [4, 64], replicated, may hold values from 0 to 62, as said below
- accepted_nodes: int32 [4, 8], replicated, may hold values from 0 to 62, as said below
- accepted_count: int32 [4], replicated, may hold values from 1 to 8, as said below
Outputs:
- projected: bfloat16 [256, 8192], P('kv', 'blk')
- new_cache_keys: bfloat16 [4, 4096, 1024], P(None, 'blk', 'kv')
- new_cache_values: bfloat16 [4, 4096, 1024], P(None, 'blk', 'kv')
The draws below stay inside these ranges and needn't reach their ends.
Inputs may be any that keep to these rules, and one draw needn't show every extreme that they name: `lengths`: some request has exactly 4088, some exactly 256. parents[r, 0] = 0 and parents[r, i] < i for i >= 1. accepted_nodes[r, 0] = 0 and accepted_nodes[r, k] is a child of accepted_nodes[r, k - 1] in request r's tree; only the first accepted_count[r] entries are used. `accepted_count`: some request has exactly 8, some exactly 1.
All inputs are finite; a program needn't handle non-finite values.
Results may differ from the reference program's by a relative error of at most 0.0055.
Values may be sent and summed in bfloat16 or wider, within the bound.
No kernel may reach another device: no remote copies, remote signals or barrier semaphores. Data moves between devices by JAX's collectives and lax.ppermute only.
A program may use at most 64 MiB of HBM per device.

```python
import math
import jax
import jax.numpy as jnp
from jax import lax

D = 8192
QUERY_HEADS = 64
KEY_VALUE_HEADS = 8
HEAD_SIZE = 128
TREE_TOKENS = 64
ACC = 8
CONTEXT_LENGTH = 4096
REQUEST_COUNT = 4
DRAFT_TOKENS = 256
BLOCK_POSITIONS = 128
N_BLK = 32


def draw_queries(key, part):
    inner_product = jax.random.fold_in(key, 11)
    attention_output = jnp.clip(jax.random.normal(inner_product, (DRAFT_TOKENS, QUERY_HEADS * HEAD_SIZE), jnp.float32), -6.0, 6.0)
    return attention_output.astype(jnp.bfloat16)


def draw_cached_key_vectors(key, part):
    inner_product = jax.random.fold_in(key, 13)
    attention_output = jnp.clip(jax.random.normal(inner_product, (REQUEST_COUNT, CONTEXT_LENGTH, KEY_VALUE_HEADS * HEAD_SIZE), jnp.float32), -6.0, 6.0)
    return attention_output.astype(jnp.bfloat16)


def pinned_ends(key, salt, lowest, highest):
    values = jax.random.randint(jax.random.fold_in(key, salt), (REQUEST_COUNT,), lowest, highest + 1)
    chosen = jax.random.permutation(jax.random.fold_in(key, salt + 1), REQUEST_COUNT)
    values = jnp.where(jnp.arange(REQUEST_COUNT) == chosen[0], highest, values)
    values = jnp.where(jnp.arange(REQUEST_COUNT) == chosen[1], lowest, values)
    return values.astype(jnp.int32)


def draw_lengths(key, part):
    return pinned_ends(key, 41, CONTEXT_LENGTH // 16, CONTEXT_LENGTH - ACC)


def draw_accepted_count(key, part):
    return pinned_ends(key, 47, 1, ACC)


def tree_draw(key):
    inner_product = jax.random.fold_in(key, 53)
    choices_base = jnp.broadcast_to(jnp.arange(1, TREE_TOKENS - 2, dtype=jnp.int32)[None, :], (REQUEST_COUNT, TREE_TOKENS - 3))
    shuffled = jax.random.permutation(jax.random.fold_in(inner_product, 1), choices_base, axis=1, independent=True)
    chosen = jnp.sort(shuffled[:, :ACC - 2], axis=1)
    path_nodes = jnp.concatenate([jnp.zeros((REQUEST_COUNT, 1), jnp.int32), chosen, jnp.full((REQUEST_COUNT, 1), TREE_TOKENS - 2, jnp.int32)], axis=1)
    upper = jnp.maximum(jnp.arange(TREE_TOKENS, dtype=jnp.int32), 1)
    parent_rows = jax.random.randint(jax.random.fold_in(inner_product, 3), (REQUEST_COUNT, TREE_TOKENS), 0, upper[None, :])
    parent_rows = parent_rows.at[:, TREE_TOKENS - 1].set(TREE_TOKENS - 2)
    request_rows = jnp.broadcast_to(jnp.arange(REQUEST_COUNT, dtype=jnp.int32)[:, None], (REQUEST_COUNT, ACC - 1))
    parent_rows = parent_rows.at[request_rows, path_nodes[:, 1:]].set(path_nodes[:, :-1])
    return (parent_rows.astype(jnp.int32), path_nodes.astype(jnp.int32))


def draw_parents(key, part):
    return tree_draw(key)[0]


def draw_accepted_nodes(key, part):
    return tree_draw(key)[1]


def block_levels(own_key, shape, cuts, least, high):
    gain, own = 1.0, jax.random.fold_in(own_key, 6)
    for axis_at, parts in cuts:
        draws = jnp.exp(jax.random.uniform(jax.random.fold_in(own, axis_at), (parts,), jnp.float32, least / len(cuts), high / len(cuts)))
        gain = gain * jnp.repeat(draws, shape[axis_at] // parts).reshape([-1 if axis == axis_at else 1 for axis in range(len(shape))])
    return gain


def normal_values(key, shape, width, bound, shards=(), held_as=jnp.bfloat16):
    loudness = block_levels(key, shape, shards, -0.22, 0.18) if shards else 1.0
    entries = jax.random.normal(key, shape, jnp.float32) * width * loudness
    return jnp.minimum(jnp.maximum(entries, -bound), bound).astype(held_as)


def setup_inputs(seed: int = 0) -> dict:
    seeds = jax.random.split(jax.random.key(seed), 11)
    queries = draw_queries(jax.random.fold_in(seeds[10], 71), 0)
    draft_token_keys = normal_values(seeds[1], (DRAFT_TOKENS, KEY_VALUE_HEADS * HEAD_SIZE), 3.0, 15.0, ((0, 32), (1, 8)))
    draft_token_values = normal_values(seeds[2], (DRAFT_TOKENS, KEY_VALUE_HEADS * HEAD_SIZE), 1.0, 6.0, ((0, 32), (1, 8)))
    cached_key_vectors = draw_cached_key_vectors(jax.random.fold_in(seeds[10], 71), 0)
    cached_value_vectors = normal_values(seeds[4], (REQUEST_COUNT, CONTEXT_LENGTH, KEY_VALUE_HEADS * HEAD_SIZE), 1.0, 6.0, ((1, 32), (2, 8)))
    out_weight = normal_values(seeds[5], (QUERY_HEADS * HEAD_SIZE, D), (QUERY_HEADS * HEAD_SIZE // 64) ** -0.5, 0.5, ((0, 8), (1, 32)))
    lengths = draw_lengths(jax.random.fold_in(seeds[10], 71), 0)
    parents = draw_parents(jax.random.fold_in(seeds[10], 71), 0)
    accepted_nodes = draw_accepted_nodes(jax.random.fold_in(seeds[10], 71), 0)
    accepted_count = draw_accepted_count(jax.random.fold_in(seeds[10], 71), 0)
    return {"queries": queries, "draft_token_keys": draft_token_keys, "draft_token_values": draft_token_values, "cached_key_vectors": cached_key_vectors, "cached_value_vectors": cached_value_vectors, "out_weight": out_weight, "lengths": lengths, "parents": parents, "accepted_nodes": accepted_nodes, "accepted_count": accepted_count}


NEG_FLOOR = -1e+30

def ancestors(parent_rows):
    node_ids = jnp.arange(TREE_TOKENS, dtype=jnp.int32)
    parent_link = ((parent_rows[:, :, None] == node_ids[None, None, :]) & (node_ids[None, :, None] >= 1)).astype(jnp.float32)
    reachable = jnp.eye(TREE_TOKENS, dtype=jnp.float32)[None] + parent_link
    for doubling in range((TREE_TOKENS - 1).bit_length()):
        reachable = jnp.minimum(reachable + jnp.einsum('rij,rjk->rik', reachable, reachable, precision=lax.Precision.HIGHEST), 1.0)
    return reachable

def partial_softmax(query_vectors, key_rows, value_rows, usable, score_scale):
    scores = jnp.einsum('rtkgh,rbpkh->brkgtp', query_vectors.astype(jnp.float32), key_rows.astype(jnp.float32)) * score_scale
    scores = jnp.where(usable, scores, NEG_FLOOR)
    peak_score = lax.optimization_barrier(jnp.max(scores, axis=-1))
    weights = jnp.where(usable, jnp.exp(scores - peak_score[..., None]), 0.0)
    weight_sum = lax.optimization_barrier(jnp.sum(weights, axis=-1))
    rounded = lax.optimization_barrier(weights.astype(jnp.bfloat16))
    weighted = jnp.einsum('brkgtp,rbpkh->brtkgh', rounded.astype(jnp.float32), value_rows.astype(jnp.float32))
    block_count, req_count, kv_count, query_group_width, row_count = peak_score.shape
    weighted = weighted.reshape(block_count, req_count * row_count, kv_count * query_group_width * value_rows.shape[-1])
    peak_score = peak_score.transpose(0, 1, 4, 2, 3).reshape(block_count, req_count * row_count, kv_count * query_group_width)
    weight_sum = weight_sum.transpose(0, 1, 4, 2, 3).reshape(block_count, req_count * row_count, kv_count * query_group_width)
    return (weighted, peak_score, weight_sum)

def merge_parts(cache_part, draft_part, head_dim):
    cache_out, cache_peak, cache_sum = cache_part
    draft_out, draft_peak, draft_sum = draft_part
    cache_out = cache_out.astype(jnp.float32)
    overall = jnp.maximum(lax.optimization_barrier(jnp.max(cache_peak, axis=0)), draft_peak[0])
    cache_factor = jnp.exp(cache_peak - overall[None])
    draft_factor = jnp.exp(draft_peak[0] - overall)
    denominator = lax.optimization_barrier(jnp.sum(cache_factor * cache_sum, axis=0)) + draft_factor * draft_sum[0]
    block_count, row_count, head_count = cache_peak.shape
    numerator = lax.optimization_barrier(jnp.sum(cache_factor[..., None] * cache_out.reshape(block_count, row_count, head_count, head_dim), axis=0))
    numerator = numerator + draft_factor[..., None] * draft_out[0].reshape(row_count, head_count, head_dim)
    return (numerator / denominator[..., None]).reshape(row_count, head_count * head_dim).astype(jnp.bfloat16)

def reference(queries, draft_token_keys, draft_token_values, cached_key_vectors, cached_value_vectors, out_weight, lengths, parents, accepted_nodes, accepted_count):
    query_group_width = QUERY_HEADS // KEY_VALUE_HEADS
    score_scale = 1.0 / math.sqrt(HEAD_SIZE)
    positions = jnp.arange(CONTEXT_LENGTH, dtype=jnp.int32).reshape(N_BLK, 1, 1, 1, 1, BLOCK_POSITIONS)

    def one_request(request_number):
        leading_row = request_number * TREE_TOKENS
        query_vectors = lax.dynamic_slice_in_dim(queries, leading_row, TREE_TOKENS, 0).reshape(1, TREE_TOKENS, KEY_VALUE_HEADS, query_group_width, HEAD_SIZE)
        request_tree_keys = lax.dynamic_slice_in_dim(draft_token_keys, leading_row, TREE_TOKENS, 0).reshape(1, 1, TREE_TOKENS, KEY_VALUE_HEADS, HEAD_SIZE)
        request_tree_values = lax.dynamic_slice_in_dim(draft_token_values, leading_row, TREE_TOKENS, 0).reshape(1, 1, TREE_TOKENS, KEY_VALUE_HEADS, HEAD_SIZE)
        keys_of_block = lax.dynamic_index_in_dim(cached_key_vectors, request_number, 0, False).reshape(1, N_BLK, BLOCK_POSITIONS, KEY_VALUE_HEADS, HEAD_SIZE)
        values_of_block = lax.dynamic_index_in_dim(cached_value_vectors, request_number, 0, False).reshape(1, N_BLK, BLOCK_POSITIONS, KEY_VALUE_HEADS, HEAD_SIZE)
        length = lax.dynamic_index_in_dim(lengths, request_number, 0, False)
        parent_rows = lax.dynamic_slice_in_dim(parents, request_number, 1, 0)
        reachable = ancestors(parent_rows)
        cache_out, cache_peak, cache_sum = partial_softmax(query_vectors, keys_of_block, values_of_block, positions < length, score_scale)
        cache_out = lax.optimization_barrier(cache_out.astype(jnp.bfloat16))
        draft_usable = (reachable > 0.5)[None, :, None, None, :, :]
        draft_part = partial_softmax(query_vectors, request_tree_keys, request_tree_values, draft_usable, score_scale)
        return merge_parts((cache_out, cache_peak, cache_sum), draft_part, HEAD_SIZE)
    attention = lax.map(one_request, jnp.arange(REQUEST_COUNT, dtype=jnp.int32)).reshape(DRAFT_TOKENS, QUERY_HEADS * HEAD_SIZE)
    projected = jnp.dot(attention, out_weight, preferred_element_type=jnp.float32).astype(jnp.bfloat16)
    offset = jnp.arange(CONTEXT_LENGTH, dtype=jnp.int32)[None, :] - lengths[:, None]
    written = (offset >= 0) & (offset < accepted_count[:, None])
    slot_index = jnp.clip(offset, 0, ACC - 1).astype(jnp.int32)
    node_ids = jnp.take_along_axis(accepted_nodes, slot_index, axis=1)
    source_rows = (jnp.arange(REQUEST_COUNT, dtype=jnp.int32)[:, None] * TREE_TOKENS + node_ids).astype(jnp.int32)
    new_cache_keys = jnp.where(written[:, :, None], draft_token_keys[source_rows], cached_key_vectors)
    new_cache_values = jnp.where(written[:, :, None], draft_token_values[source_rows], cached_value_vectors)
    return (projected, new_cache_keys, new_cache_values)
```

```python
import math

import jax
import jax.numpy as jnp
from jax import lax
from jax.sharding import PartitionSpec as P

HEAD_SIZE = 128
TREE_TOKENS = 64
ACC = 8


NEG_FLOOR = -1e30


def ancestors(parent_rows):
    node_ids = jnp.arange(TREE_TOKENS, dtype=jnp.int32)
    parent_link = (
        (parent_rows[:, :, None] == node_ids[None, None, :]) & (node_ids[None, :, None] >= 1)
    ).astype(jnp.float32)
    reachable = jnp.eye(TREE_TOKENS, dtype=jnp.float32)[None] + parent_link
    for doubling in range((TREE_TOKENS - 1).bit_length()):
        reachable = jnp.minimum(
            reachable
            + jnp.einsum("rij,rjk->rik", reachable, reachable, precision=lax.Precision.HIGHEST),
            1.0,
        )
    return reachable


def partial_softmax(query_vectors, key_rows, value_rows, usable, score_scale):
    scores = (
        jnp.einsum(
            "rtkgh,rbpkh->brkgtp", query_vectors, key_rows, preferred_element_type=jnp.float32
        )
        * score_scale
    )
    scores = jnp.where(usable, scores, NEG_FLOOR)
    peak_score = jnp.max(scores, axis=-1)
    weights = jnp.where(usable, jnp.exp(scores - peak_score[..., None]), 0.0)
    weight_sum = jnp.sum(weights, axis=-1)
    weighted = jnp.einsum(
        "brkgtp,rbpkh->brtkgh",
        weights.astype(jnp.bfloat16),
        value_rows,
        preferred_element_type=jnp.float32,
    )
    block_count, req_count, kv_count, query_group_width, row_count = peak_score.shape
    weighted = weighted.reshape(
        block_count, req_count * row_count, kv_count * query_group_width * value_rows.shape[-1]
    )
    peak_score = peak_score.transpose(0, 1, 4, 2, 3).reshape(
        block_count, req_count * row_count, kv_count * query_group_width
    )
    weight_sum = weight_sum.transpose(0, 1, 4, 2, 3).reshape(
        block_count, req_count * row_count, kv_count * query_group_width
    )
    return (weighted, peak_score, weight_sum)


def merge_parts(cache_part, draft_part, head_dim):
    cache_out, cache_peak, cache_sum = cache_part
    draft_out, draft_peak, draft_sum = draft_part
    cache_out = cache_out.astype(jnp.float32)
    overall = jnp.maximum(jnp.max(cache_peak, axis=0), draft_peak[0])
    cache_factor = jnp.exp(cache_peak - overall[None])
    draft_factor = jnp.exp(draft_peak[0] - overall)
    denominator = jnp.sum(cache_factor * cache_sum, axis=0) + draft_factor * draft_sum[0]
    block_count, row_count, head_count = cache_peak.shape
    numerator = jnp.sum(
        cache_factor[..., None] * cache_out.reshape(block_count, row_count, head_count, head_dim),
        axis=0,
    )
    numerator = numerator + draft_factor[..., None] * draft_out[0].reshape(
        row_count, head_count, head_dim
    )
    return (
        (numerator / denominator[..., None])
        .reshape(row_count, head_count * head_dim)
        .astype(jnp.bfloat16)
    )


def place_rows(sources, slot_index, written, cache_rows):
    slot_ids = jnp.arange(sources.shape[1], dtype=jnp.int32)
    selector = ((slot_index[:, :, None] == slot_ids[None, None, :]) & written[:, :, None]).astype(
        jnp.bfloat16
    )
    placed = jnp.einsum(
        "rps,rsc->rpc", selector, sources, preferred_element_type=jnp.float32
    ).astype(jnp.bfloat16)
    return jnp.where(written[:, :, None], placed, cache_rows)


def gather_rows(block, axis_name):
    count = lax.axis_size(axis_name)
    spread = jnp.broadcast_to(block[None], (count,) + block.shape)
    moved = lax.all_to_all(spread, axis_name, split_axis=0, concat_axis=0, tiled=True)
    return moved.reshape((count * block.shape[0],) + block.shape[1:])


def on_device(
    queries,
    draft_token_keys,
    draft_token_values,
    cached_key_vectors,
    cached_value_vectors,
    out_weight,
    lengths,
    parents,
    accepted_nodes,
    accepted_count,
):
    block_count = lax.axis_size("blk")
    kv_count = lax.axis_size("kv")
    my_block = lax.axis_index("blk")
    rows_dev, width_q = queries.shape
    requests = lengths.shape[0]
    cache_width = cached_key_vectors.shape[2]
    kv_local = cache_width // HEAD_SIZE
    query_group_width = width_q // (kv_local * HEAD_SIZE)
    block_len = cached_key_vectors.shape[1]
    score_scale = 1.0 / math.sqrt(HEAD_SIZE)
    leading_row = my_block * rows_dev
    my_request = leading_row // TREE_TOKENS
    node_start = leading_row - my_request * TREE_TOKENS
    local_queries = queries.reshape(1, rows_dev, kv_local, query_group_width, HEAD_SIZE)
    packed = gather_rows(
        jnp.concatenate([queries, draft_token_keys, draft_token_values], axis=1), "blk"
    )
    every_query = packed[:, :width_q]
    gathered_keys = packed[:, width_q : width_q + cache_width]
    gathered_values = packed[:, width_q + cache_width :]
    tree_keys = lax.dynamic_slice_in_dim(
        gathered_keys, my_request * TREE_TOKENS, TREE_TOKENS, 0
    ).reshape(1, 1, TREE_TOKENS, kv_local, HEAD_SIZE)
    tree_values = lax.dynamic_slice_in_dim(
        gathered_values, my_request * TREE_TOKENS, TREE_TOKENS, 0
    ).reshape(1, 1, TREE_TOKENS, kv_local, HEAD_SIZE)
    reachable = ancestors(lax.dynamic_slice_in_dim(parents, my_request, 1, 0))
    own_reach = lax.dynamic_slice_in_dim(reachable, node_start, rows_dev, 1)
    draft_usable = (own_reach > 0.5)[None, :, None, None, :, :]
    draft_part = partial_softmax(local_queries, tree_keys, tree_values, draft_usable, score_scale)
    all_queries = every_query.reshape(requests, TREE_TOKENS, kv_local, query_group_width, HEAD_SIZE)
    positions = my_block * block_len + jnp.arange(block_len, dtype=jnp.int32)
    usable = (positions[None, :] < lengths[:, None])[None, :, None, None, None, :]
    local_out, local_peak, local_sum = partial_softmax(
        all_queries,
        cached_key_vectors.reshape(requests, 1, block_len, kv_local, HEAD_SIZE),
        cached_value_vectors.reshape(requests, 1, block_len, kv_local, HEAD_SIZE),
        usable,
        score_scale,
    )
    moved_out = lax.all_to_all(
        local_out[0].astype(jnp.bfloat16), "blk", split_axis=0, concat_axis=0, tiled=True
    )
    head_count = local_peak.shape[-1]
    moved_stats = lax.all_to_all(
        jnp.concatenate([local_peak[0], local_sum[0]], axis=1),
        "blk",
        split_axis=0,
        concat_axis=0,
        tiled=True,
    ).reshape(block_count, rows_dev, 2 * head_count)
    cache_part = (
        moved_out.reshape(block_count, rows_dev, -1),
        moved_stats[..., :head_count],
        moved_stats[..., head_count:],
    )
    attention = merge_parts(cache_part, draft_part, HEAD_SIZE)
    every_row = gather_rows(attention, "blk")
    partial = jnp.dot(every_row, out_weight, preferred_element_type=jnp.float32)
    out_rows = partial.shape[0] // kv_count
    arrived = lax.all_to_all(
        partial.reshape(kv_count, out_rows, partial.shape[1]),
        "kv",
        split_axis=0,
        concat_axis=0,
        tiled=True,
    )
    projected = jnp.sum(arrived, axis=0).astype(jnp.bfloat16)
    positions_here = my_block * block_len + jnp.arange(block_len, dtype=jnp.int32)
    offset = positions_here[None, :] - lengths[:, None]
    written = (offset >= 0) & (offset < accepted_count[:, None])
    slot_match = offset[:, :, None] == jnp.arange(ACC, dtype=jnp.int32)[None, None, :]
    node_ids = jnp.sum(jnp.where(slot_match, accepted_nodes[:, None, :], 0), axis=-1)
    new_cache_keys = place_rows(
        gathered_keys.reshape(requests, TREE_TOKENS, cache_width),
        node_ids,
        written,
        cached_key_vectors,
    )
    new_cache_values = place_rows(
        gathered_values.reshape(requests, TREE_TOKENS, cache_width),
        node_ids,
        written,
        cached_value_vectors,
    )
    return (projected, new_cache_keys, new_cache_values)


def solution(mesh):
    return jax.shard_map(
        on_device,
        mesh=mesh,
        in_specs=(
            P("blk", "kv"),
            P("blk", "kv"),
            P("blk", "kv"),
            P(None, "blk", "kv"),
            P(None, "blk", "kv"),
            P("kv", "blk"),
            P(),
            P(),
            P(),
            P(),
        ),
        out_specs=(P("kv", "blk"), P(None, "blk", "kv"), P(None, "blk", "kv")),
        check_vma=False,
    )
```

```python
import math

import jax
import jax.numpy as jnp
from jax import lax
from jax.sharding import PartitionSpec as P

HEAD_SIZE = 128
TREE_TOKENS = 64
ACC = 8


NEG_FLOOR = -1e30


def ancestors(parent_rows):
    node_ids = jnp.arange(TREE_TOKENS, dtype=jnp.int32)
    parent_link = (
        (parent_rows[:, :, None] == node_ids[None, None, :]) & (node_ids[None, :, None] >= 1)
    ).astype(jnp.float32)
    reachable = jnp.eye(TREE_TOKENS, dtype=jnp.float32)[None] + parent_link
    for doubling in range((TREE_TOKENS - 1).bit_length()):
        reachable = jnp.minimum(
            reachable
            + jnp.einsum("rij,rjk->rik", reachable, reachable, precision=lax.Precision.HIGHEST),
            1.0,
        )
    return reachable


def partial_softmax(query_vectors, key_rows, value_rows, usable, score_scale):
    scores = (
        jnp.einsum(
            "rtkgh,rbpkh->brkgtp", query_vectors, key_rows, preferred_element_type=jnp.float32
        )
        * score_scale
    )
    scores = jnp.where(usable, scores, NEG_FLOOR)
    peak_score = jnp.max(scores, axis=-1)
    weights = jnp.where(usable, jnp.exp(scores - peak_score[..., None]), 0.0)
    weight_sum = jnp.sum(weights, axis=-1)
    weighted = jnp.einsum(
        "brkgtp,rbpkh->brtkgh",
        weights.astype(jnp.bfloat16),
        value_rows,
        preferred_element_type=jnp.float32,
    )
    block_count, req_count, kv_count, query_group_width, row_count = peak_score.shape
    weighted = weighted.reshape(
        block_count, req_count * row_count, kv_count * query_group_width * value_rows.shape[-1]
    )
    peak_score = peak_score.transpose(0, 1, 4, 2, 3).reshape(
        block_count, req_count * row_count, kv_count * query_group_width
    )
    weight_sum = weight_sum.transpose(0, 1, 4, 2, 3).reshape(
        block_count, req_count * row_count, kv_count * query_group_width
    )
    return (weighted, peak_score, weight_sum)


def merge_parts(cache_part, draft_part, head_dim):
    cache_out, cache_peak, cache_sum = cache_part
    draft_out, draft_peak, draft_sum = draft_part
    cache_out = cache_out.astype(jnp.float32)
    overall = jnp.maximum(jnp.max(cache_peak, axis=0), draft_peak[0])
    cache_factor = jnp.exp(cache_peak - overall[None])
    draft_factor = jnp.exp(draft_peak[0] - overall)
    denominator = jnp.sum(cache_factor * cache_sum, axis=0) + draft_factor * draft_sum[0]
    block_count, row_count, head_count = cache_peak.shape
    numerator = jnp.sum(
        cache_factor[..., None] * cache_out.reshape(block_count, row_count, head_count, head_dim),
        axis=0,
    )
    numerator = numerator + draft_factor[..., None] * draft_out[0].reshape(
        row_count, head_count, head_dim
    )
    return (
        (numerator / denominator[..., None])
        .reshape(row_count, head_count * head_dim)
        .astype(jnp.bfloat16)
    )


def place_rows(sources, slot_index, written, cache_rows):
    slot_ids = jnp.arange(sources.shape[1], dtype=jnp.int32)
    selector = ((slot_index[:, :, None] == slot_ids[None, None, :]) & written[:, :, None]).astype(
        jnp.bfloat16
    )
    placed = jnp.einsum(
        "rps,rsc->rpc", selector, sources, preferred_element_type=jnp.float32
    ).astype(jnp.bfloat16)
    return jnp.where(written[:, :, None], placed, cache_rows)


def shifted(block, axis_name, shift):
    count = lax.axis_size(axis_name)
    return lax.ppermute(block, axis_name, [(i, (i + shift) % count) for i in range(count)])


def gather_rows(block, axis_name):
    count = lax.axis_size(axis_name)
    me = lax.axis_index(axis_name)
    pieces = [block] + [shifted(block, axis_name, count - k) for k in range(1, count)]
    stacked = jnp.concatenate(pieces, axis=0)
    return jnp.roll(stacked, me * block.shape[0], axis=0)


def spread_rows(rows, axis_name):
    count = lax.axis_size(axis_name)
    me = lax.axis_index(axis_name)
    chunk = rows.shape[0] // count
    ahead = jnp.roll(rows, -me * chunk, axis=0)
    pieces = [ahead[:chunk]] + [
        shifted(ahead[k * chunk : (k + 1) * chunk], axis_name, k) for k in range(1, count)
    ]
    return jnp.stack(pieces, axis=0)


def on_device(
    queries,
    draft_token_keys,
    draft_token_values,
    cached_key_vectors,
    cached_value_vectors,
    out_weight,
    lengths,
    parents,
    accepted_nodes,
    accepted_count,
):
    block_count = lax.axis_size("blk")
    kv_count = lax.axis_size("kv")
    my_block = lax.axis_index("blk")
    rows_dev, width_q = queries.shape
    requests = lengths.shape[0]
    cache_width = cached_key_vectors.shape[2]
    kv_local = cache_width // HEAD_SIZE
    query_group_width = width_q // (kv_local * HEAD_SIZE)
    block_len = cached_key_vectors.shape[1]
    score_scale = 1.0 / math.sqrt(HEAD_SIZE)
    leading_row = my_block * rows_dev
    my_request = leading_row // TREE_TOKENS
    node_start = leading_row - my_request * TREE_TOKENS
    local_queries = queries.reshape(1, rows_dev, kv_local, query_group_width, HEAD_SIZE)
    packed = gather_rows(
        jnp.concatenate([queries, draft_token_keys, draft_token_values], axis=1), "blk"
    )
    every_query = packed[:, :width_q]
    gathered_keys = packed[:, width_q : width_q + cache_width]
    gathered_values = packed[:, width_q + cache_width :]
    tree_keys = lax.dynamic_slice_in_dim(
        gathered_keys, my_request * TREE_TOKENS, TREE_TOKENS, 0
    ).reshape(1, 1, TREE_TOKENS, kv_local, HEAD_SIZE)
    tree_values = lax.dynamic_slice_in_dim(
        gathered_values, my_request * TREE_TOKENS, TREE_TOKENS, 0
    ).reshape(1, 1, TREE_TOKENS, kv_local, HEAD_SIZE)
    reachable = ancestors(lax.dynamic_slice_in_dim(parents, my_request, 1, 0))
    own_reach = lax.dynamic_slice_in_dim(reachable, node_start, rows_dev, 1)
    draft_usable = (own_reach > 0.5)[None, :, None, None, :, :]
    draft_part = partial_softmax(local_queries, tree_keys, tree_values, draft_usable, score_scale)
    all_queries = every_query.reshape(requests, TREE_TOKENS, kv_local, query_group_width, HEAD_SIZE)
    positions = my_block * block_len + jnp.arange(block_len, dtype=jnp.int32)
    usable = (positions[None, :] < lengths[:, None])[None, :, None, None, None, :]
    local_out, local_peak, local_sum = partial_softmax(
        all_queries,
        cached_key_vectors.reshape(requests, 1, block_len, kv_local, HEAD_SIZE),
        cached_value_vectors.reshape(requests, 1, block_len, kv_local, HEAD_SIZE),
        usable,
        score_scale,
    )
    head_count = local_peak.shape[-1]
    moved_out = spread_rows(local_out[0].astype(jnp.bfloat16), "blk")
    moved_stats = spread_rows(jnp.concatenate([local_peak[0], local_sum[0]], axis=1), "blk")
    cache_part = (
        moved_out.reshape(block_count, rows_dev, -1),
        moved_stats[..., :head_count],
        moved_stats[..., head_count:],
    )
    attention = merge_parts(cache_part, draft_part, HEAD_SIZE)
    every_row = gather_rows(attention, "blk")
    partial = jnp.dot(every_row, out_weight, preferred_element_type=jnp.float32)
    out_rows = partial.shape[0] // kv_count
    arrived = lax.all_to_all(
        partial.reshape(kv_count, out_rows, partial.shape[1]),
        "kv",
        split_axis=0,
        concat_axis=0,
        tiled=True,
    )
    projected = jnp.sum(arrived, axis=0).astype(jnp.bfloat16)
    positions_here = my_block * block_len + jnp.arange(block_len, dtype=jnp.int32)
    offset = positions_here[None, :] - lengths[:, None]
    written = (offset >= 0) & (offset < accepted_count[:, None])
    slot_match = offset[:, :, None] == jnp.arange(ACC, dtype=jnp.int32)[None, None, :]
    node_ids = jnp.sum(jnp.where(slot_match, accepted_nodes[:, None, :], 0), axis=-1)
    new_cache_keys = place_rows(
        gathered_keys.reshape(requests, TREE_TOKENS, cache_width),
        node_ids,
        written,
        cached_key_vectors,
    )
    new_cache_values = place_rows(
        gathered_values.reshape(requests, TREE_TOKENS, cache_width),
        node_ids,
        written,
        cached_value_vectors,
    )
    return (projected, new_cache_keys, new_cache_values)


def solution(mesh):
    return jax.shard_map(
        on_device,
        mesh=mesh,
        in_specs=(
            P("blk", "kv"),
            P("blk", "kv"),
            P("blk", "kv"),
            P(None, "blk", "kv"),
            P(None, "blk", "kv"),
            P("kv", "blk"),
            P(),
            P(),
            P(),
            P(),
        ),
        out_specs=(P("kv", "blk"), P(None, "blk", "kv"), P(None, "blk", "kv")),
        check_vma=False,
    )
```

```python
import math

import jax
import jax.numpy as jnp
from jax import lax
from jax.sharding import PartitionSpec as P

HEAD_SIZE = 128
TREE_TOKENS = 64
ACC = 8


NEG_FLOOR = -1e30


def ancestors(parent_rows):
    node_ids = jnp.arange(TREE_TOKENS, dtype=jnp.int32)
    parent_link = (
        (parent_rows[:, :, None] == node_ids[None, None, :]) & (node_ids[None, :, None] >= 1)
    ).astype(jnp.float32)
    reachable = jnp.eye(TREE_TOKENS, dtype=jnp.float32)[None] + parent_link
    for doubling in range((TREE_TOKENS - 1).bit_length()):
        reachable = jnp.minimum(
            reachable
            + jnp.einsum("rij,rjk->rik", reachable, reachable, precision=lax.Precision.HIGHEST),
            1.0,
        )
    return reachable


def partial_softmax(query_vectors, key_rows, value_rows, usable, score_scale):
    scores = (
        jnp.einsum(
            "rtkgh,rbpkh->brkgtp", query_vectors, key_rows, preferred_element_type=jnp.float32
        )
        * score_scale
    )
    scores = jnp.where(usable, scores, NEG_FLOOR)
    peak_score = jnp.max(scores, axis=-1)
    weights = jnp.where(usable, jnp.exp(scores - peak_score[..., None]), 0.0)
    weight_sum = jnp.sum(weights, axis=-1)
    weighted = jnp.einsum(
        "brkgtp,rbpkh->brtkgh",
        weights.astype(jnp.bfloat16),
        value_rows,
        preferred_element_type=jnp.float32,
    )
    block_count, req_count, kv_count, query_group_width, row_count = peak_score.shape
    weighted = weighted.reshape(
        block_count, req_count * row_count, kv_count * query_group_width * value_rows.shape[-1]
    )
    peak_score = peak_score.transpose(0, 1, 4, 2, 3).reshape(
        block_count, req_count * row_count, kv_count * query_group_width
    )
    weight_sum = weight_sum.transpose(0, 1, 4, 2, 3).reshape(
        block_count, req_count * row_count, kv_count * query_group_width
    )
    return (weighted, peak_score, weight_sum)


def merge_parts(cache_part, draft_part, head_dim):
    cache_out, cache_peak, cache_sum = cache_part
    draft_out, draft_peak, draft_sum = draft_part
    cache_out = cache_out.astype(jnp.float32)
    overall = jnp.maximum(jnp.max(cache_peak, axis=0), draft_peak[0])
    cache_factor = jnp.exp(cache_peak - overall[None])
    draft_factor = jnp.exp(draft_peak[0] - overall)
    denominator = jnp.sum(cache_factor * cache_sum, axis=0) + draft_factor * draft_sum[0]
    block_count, row_count, head_count = cache_peak.shape
    numerator = jnp.sum(
        cache_factor[..., None] * cache_out.reshape(block_count, row_count, head_count, head_dim),
        axis=0,
    )
    numerator = numerator + draft_factor[..., None] * draft_out[0].reshape(
        row_count, head_count, head_dim
    )
    return (
        (numerator / denominator[..., None])
        .reshape(row_count, head_count * head_dim)
        .astype(jnp.bfloat16)
    )


def place_rows(sources, slot_index, written, cache_rows):
    slot_ids = jnp.arange(sources.shape[1], dtype=jnp.int32)
    selector = ((slot_index[:, :, None] == slot_ids[None, None, :]) & written[:, :, None]).astype(
        jnp.bfloat16
    )
    placed = jnp.einsum(
        "rps,rsc->rpc", selector, sources, preferred_element_type=jnp.float32
    ).astype(jnp.bfloat16)
    return jnp.where(written[:, :, None], placed, cache_rows)


def gather_rows(block, axis_name):
    count = lax.axis_size(axis_name)
    spread = jnp.broadcast_to(block[None], (count,) + block.shape)
    moved = lax.all_to_all(spread, axis_name, split_axis=0, concat_axis=0, tiled=True)
    return moved.reshape((count * block.shape[0],) + block.shape[1:])


def on_device(
    queries,
    draft_token_keys,
    draft_token_values,
    cached_key_vectors,
    cached_value_vectors,
    out_weight,
    lengths,
    parents,
    accepted_nodes,
    accepted_count,
):
    block_count = lax.axis_size("blk")
    kv_count = lax.axis_size("kv")
    my_block = lax.axis_index("blk")
    rows_dev, width_q = queries.shape
    requests = lengths.shape[0]
    cache_width = cached_key_vectors.shape[2]
    kv_local = cache_width // HEAD_SIZE
    query_group_width = width_q // (kv_local * HEAD_SIZE)
    block_len = cached_key_vectors.shape[1]
    score_scale = 1.0 / math.sqrt(HEAD_SIZE)
    leading_row = my_block * rows_dev
    my_request = leading_row // TREE_TOKENS
    node_start = leading_row - my_request * TREE_TOKENS
    local_queries = queries.reshape(1, rows_dev, kv_local, query_group_width, HEAD_SIZE)
    packed = gather_rows(
        jnp.concatenate([queries, draft_token_keys, draft_token_values], axis=1), "blk"
    )
    every_query = packed[:, :width_q]
    gathered_keys = packed[:, width_q : width_q + cache_width]
    gathered_values = packed[:, width_q + cache_width :]
    tree_keys = lax.dynamic_slice_in_dim(
        gathered_keys, my_request * TREE_TOKENS, TREE_TOKENS, 0
    ).reshape(1, 1, TREE_TOKENS, kv_local, HEAD_SIZE)
    tree_values = lax.dynamic_slice_in_dim(
        gathered_values, my_request * TREE_TOKENS, TREE_TOKENS, 0
    ).reshape(1, 1, TREE_TOKENS, kv_local, HEAD_SIZE)
    reachable = ancestors(lax.dynamic_slice_in_dim(parents, my_request, 1, 0))
    own_reach = lax.dynamic_slice_in_dim(reachable, node_start, rows_dev, 1)
    draft_usable = (own_reach > 0.5)[None, :, None, None, :, :]
    draft_part = partial_softmax(local_queries, tree_keys, tree_values, draft_usable, score_scale)
    all_queries = every_query.reshape(requests, TREE_TOKENS, kv_local, query_group_width, HEAD_SIZE)
    positions = my_block * block_len + jnp.arange(block_len, dtype=jnp.int32)
    usable = (positions[None, :] < lengths[:, None])[None, :, None, None, None, :]
    local_out, local_peak, local_sum = partial_softmax(
        all_queries,
        cached_key_vectors.reshape(requests, 1, block_len, kv_local, HEAD_SIZE),
        cached_value_vectors.reshape(requests, 1, block_len, kv_local, HEAD_SIZE),
        usable,
        score_scale,
    )
    head_count = local_peak.shape[-1]
    stats = jnp.concatenate([local_peak[0], local_sum[0]], axis=1)
    hi = lax.reduce_precision(stats, exponent_bits=8, mantissa_bits=7)
    rest = stats - hi
    mid = lax.reduce_precision(rest, exponent_bits=8, mantissa_bits=7)
    lo = rest - mid
    width_out = local_out.shape[-1]
    packed_out = jnp.concatenate(
        [local_out[0].astype(jnp.bfloat16)]
        + [part.astype(jnp.bfloat16) for part in (hi, mid, lo)],
        axis=1,
    )
    moved = lax.all_to_all(packed_out, "blk", split_axis=0, concat_axis=0, tiled=True)
    moved = moved.reshape(block_count, rows_dev, -1)
    parts = [
        moved[..., width_out + j * 2 * head_count : width_out + (j + 1) * 2 * head_count].astype(
            jnp.float32
        )
        for j in range(3)
    ]
    moved_stats = (parts[0] + parts[1]) + parts[2]
    cache_part = (
        moved[..., :width_out],
        moved_stats[..., :head_count],
        moved_stats[..., head_count:],
    )
    attention = merge_parts(cache_part, draft_part, HEAD_SIZE)
    every_row = gather_rows(attention, "blk")
    partial = jnp.dot(every_row, out_weight, preferred_element_type=jnp.float32)
    out_rows = partial.shape[0] // kv_count
    arrived = lax.all_to_all(
        partial.reshape(kv_count, out_rows, partial.shape[1]),
        "kv",
        split_axis=0,
        concat_axis=0,
        tiled=True,
    )
    projected = jnp.sum(arrived, axis=0).astype(jnp.bfloat16)
    positions_here = my_block * block_len + jnp.arange(block_len, dtype=jnp.int32)
    offset = positions_here[None, :] - lengths[:, None]
    written = (offset >= 0) & (offset < accepted_count[:, None])
    slot_match = offset[:, :, None] == jnp.arange(ACC, dtype=jnp.int32)[None, None, :]
    node_ids = jnp.sum(jnp.where(slot_match, accepted_nodes[:, None, :], 0), axis=-1)
    new_cache_keys = place_rows(
        gathered_keys.reshape(requests, TREE_TOKENS, cache_width),
        node_ids,
        written,
        cached_key_vectors,
    )
    new_cache_values = place_rows(
        gathered_values.reshape(requests, TREE_TOKENS, cache_width),
        node_ids,
        written,
        cached_value_vectors,
    )
    return (projected, new_cache_keys, new_cache_values)


def solution(mesh):
    return jax.shard_map(
        on_device,
        mesh=mesh,
        in_specs=(
            P("blk", "kv"),
            P("blk", "kv"),
            P("blk", "kv"),
            P(None, "blk", "kv"),
            P(None, "blk", "kv"),
            P("kv", "blk"),
            P(),
            P(),
            P(),
            P(),
        ),
        out_specs=(P("kv", "blk"), P(None, "blk", "kv"), P(None, "blk", "kv")),
        check_vma=False,
    )
```

```python
import math

import jax
import jax.numpy as jnp
from jax import lax
from jax.sharding import PartitionSpec as P
from jax.experimental import pallas as pl
from jax.experimental.pallas import tpu as pltpu

HEAD_SIZE = 128
TREE_TOKENS = 64
ACC = 8


NEG_FLOOR = -1e30


def ancestors(parent_rows):
    node_ids = jnp.arange(TREE_TOKENS, dtype=jnp.int32)
    parent_link = (
        (parent_rows[:, :, None] == node_ids[None, None, :]) & (node_ids[None, :, None] >= 1)
    ).astype(jnp.float32)
    reachable = jnp.eye(TREE_TOKENS, dtype=jnp.float32)[None] + parent_link
    for doubling in range((TREE_TOKENS - 1).bit_length()):
        reachable = jnp.minimum(
            reachable
            + jnp.einsum("rij,rjk->rik", reachable, reachable, precision=lax.Precision.HIGHEST),
            1.0,
        )
    return reachable


def partial_softmax(query_vectors, key_rows, value_rows, usable, score_scale):
    scores = (
        jnp.einsum(
            "rtkgh,rbpkh->brkgtp", query_vectors, key_rows, preferred_element_type=jnp.float32
        )
        * score_scale
    )
    scores = jnp.where(usable, scores, NEG_FLOOR)
    peak_score = jnp.max(scores, axis=-1)
    weights = jnp.where(usable, jnp.exp(scores - peak_score[..., None]), 0.0)
    weight_sum = jnp.sum(weights, axis=-1)
    weighted = jnp.einsum(
        "brkgtp,rbpkh->brtkgh",
        weights.astype(jnp.bfloat16),
        value_rows,
        preferred_element_type=jnp.float32,
    )
    block_count, req_count, kv_count, query_group_width, row_count = peak_score.shape
    weighted = weighted.reshape(
        block_count, req_count * row_count, kv_count * query_group_width * value_rows.shape[-1]
    )
    peak_score = peak_score.transpose(0, 1, 4, 2, 3).reshape(
        block_count, req_count * row_count, kv_count * query_group_width
    )
    weight_sum = weight_sum.transpose(0, 1, 4, 2, 3).reshape(
        block_count, req_count * row_count, kv_count * query_group_width
    )
    return (weighted, peak_score, weight_sum)


def merge_parts(cache_part, draft_part, head_dim):
    cache_out, cache_peak, cache_sum = cache_part
    draft_out, draft_peak, draft_sum = draft_part
    cache_out = cache_out.astype(jnp.float32)
    overall = jnp.maximum(jnp.max(cache_peak, axis=0), draft_peak[0])
    cache_factor = jnp.exp(cache_peak - overall[None])
    draft_factor = jnp.exp(draft_peak[0] - overall)
    denominator = jnp.sum(cache_factor * cache_sum, axis=0) + draft_factor * draft_sum[0]
    block_count, row_count, head_count = cache_peak.shape
    numerator = jnp.sum(
        cache_factor[..., None] * cache_out.reshape(block_count, row_count, head_count, head_dim),
        axis=0,
    )
    numerator = numerator + draft_factor[..., None] * draft_out[0].reshape(
        row_count, head_count, head_dim
    )
    return (
        (numerator / denominator[..., None])
        .reshape(row_count, head_count * head_dim)
        .astype(jnp.bfloat16)
    )


def place_rows(sources, slot_index, written, cache_rows):
    slot_ids = jnp.arange(sources.shape[1], dtype=jnp.int32)
    selector = ((slot_index[:, :, None] == slot_ids[None, None, :]) & written[:, :, None]).astype(
        jnp.bfloat16
    )
    placed = jnp.einsum(
        "rps,rsc->rpc", selector, sources, preferred_element_type=jnp.float32
    ).astype(jnp.bfloat16)
    return jnp.where(written[:, :, None], placed, cache_rows)


def split_three(x):
    hi = x.astype(jnp.bfloat16)
    rest = x - hi.astype(jnp.float32)
    mid = rest.astype(jnp.bfloat16)
    lo = (rest - mid.astype(jnp.float32)).astype(jnp.bfloat16)
    return hi, mid, lo


def block_attention_kernel(limit_ref, q_ref, k_ref, v_ref, out_ref, stats_ref):
    requests, block_len, _ = k_ref.shape
    rows = q_ref.shape[0] // requests
    heads = q_ref.shape[1] // HEAD_SIZE
    score_scale = 1.0 / math.sqrt(HEAD_SIZE)
    for r in range(requests):
        keys = k_ref[r]
        values = v_ref[r]
        valid = lax.broadcasted_iota(jnp.int32, (rows, block_len), 1) < limit_ref[r]
        for h in range(heads):
            q = q_ref[r * rows : (r + 1) * rows, h * HEAD_SIZE : (h + 1) * HEAD_SIZE]
            scores = (
                lax.dot_general(
                    q, keys, (((1,), (1,)), ((), ())), preferred_element_type=jnp.float32
                )
                * score_scale
            )
            scores = jnp.where(valid, scores, NEG_FLOOR)
            peak = jnp.max(scores, axis=1, keepdims=True)
            weights = jnp.where(valid, jnp.exp(scores - peak), 0.0)
            total = jnp.sum(weights, axis=1, keepdims=True)
            out = jnp.dot(
                weights.astype(jnp.bfloat16), values, preferred_element_type=jnp.float32
            )
            out_ref[r * rows : (r + 1) * rows, h * HEAD_SIZE : (h + 1) * HEAD_SIZE] = out.astype(
                out_ref.dtype
            )
            stats_ref[r * rows : (r + 1) * rows, h : h + 1] = peak
            stats_ref[r * rows : (r + 1) * rows, heads + h : heads + h + 1] = total
    width = heads * HEAD_SIZE
    stats = stats_ref[...]
    for j, part in enumerate(split_three(stats)):
        out_ref[:, width + j * 2 * heads : width + (j + 1) * 2 * heads] = part


def block_attention(limit, every_query, keys, values):
    rows, width = every_query.shape
    heads = width // HEAD_SIZE
    requests, block_len, _ = keys.shape
    vmem = pl.BlockSpec(memory_space=pltpu.VMEM)
    return pl.pallas_call(
        block_attention_kernel,
        out_shape=jax.ShapeDtypeStruct((rows, width + 6 * heads), jnp.bfloat16),
        in_specs=[pl.BlockSpec(memory_space=pltpu.SMEM), vmem, vmem, vmem],
        out_specs=vmem,
        scratch_shapes=[pltpu.VMEM((rows, 2 * heads), jnp.float32)],
        cost_estimate=pl.CostEstimate(
            flops=4 * rows * heads * block_len * HEAD_SIZE,
            transcendentals=rows * heads * block_len,
            bytes_accessed=2 * (rows * width + 2 * requests * block_len * HEAD_SIZE + rows * (width + 6 * heads)),
        ),
    )(limit, every_query, keys, values)


def gather_rows(block, axis_name):
    count = lax.axis_size(axis_name)
    spread = jnp.broadcast_to(block[None], (count,) + block.shape)
    moved = lax.all_to_all(spread, axis_name, split_axis=0, concat_axis=0, tiled=True)
    return moved.reshape((count * block.shape[0],) + block.shape[1:])


def on_device(
    queries,
    draft_token_keys,
    draft_token_values,
    cached_key_vectors,
    cached_value_vectors,
    out_weight,
    lengths,
    parents,
    accepted_nodes,
    accepted_count,
):
    block_count = lax.axis_size("blk")
    kv_count = lax.axis_size("kv")
    my_block = lax.axis_index("blk")
    rows_dev, width_q = queries.shape
    requests = lengths.shape[0]
    cache_width = cached_key_vectors.shape[2]
    kv_local = cache_width // HEAD_SIZE
    query_group_width = width_q // (kv_local * HEAD_SIZE)
    block_len = cached_key_vectors.shape[1]
    score_scale = 1.0 / math.sqrt(HEAD_SIZE)
    leading_row = my_block * rows_dev
    my_request = leading_row // TREE_TOKENS
    node_start = leading_row - my_request * TREE_TOKENS
    local_queries = queries.reshape(1, rows_dev, kv_local, query_group_width, HEAD_SIZE)
    packed = gather_rows(
        jnp.concatenate([queries, draft_token_keys, draft_token_values], axis=1), "blk"
    )
    every_query = packed[:, :width_q]
    gathered_keys = packed[:, width_q : width_q + cache_width]
    gathered_values = packed[:, width_q + cache_width :]
    tree_keys = lax.dynamic_slice_in_dim(
        gathered_keys, my_request * TREE_TOKENS, TREE_TOKENS, 0
    ).reshape(1, 1, TREE_TOKENS, kv_local, HEAD_SIZE)
    tree_values = lax.dynamic_slice_in_dim(
        gathered_values, my_request * TREE_TOKENS, TREE_TOKENS, 0
    ).reshape(1, 1, TREE_TOKENS, kv_local, HEAD_SIZE)
    reachable = ancestors(lax.dynamic_slice_in_dim(parents, my_request, 1, 0))
    own_reach = lax.dynamic_slice_in_dim(reachable, node_start, rows_dev, 1)
    draft_usable = (own_reach > 0.5)[None, :, None, None, :, :]
    draft_part = partial_softmax(local_queries, tree_keys, tree_values, draft_usable, score_scale)
    limit = lengths - my_block * block_len
    packed_out = block_attention(
        limit, every_query, cached_key_vectors, cached_value_vectors
    )
    head_count = width_q // HEAD_SIZE
    width_out = width_q
    moved = lax.all_to_all(packed_out, "blk", split_axis=0, concat_axis=0, tiled=True)
    moved = moved.reshape(block_count, rows_dev, -1)
    parts = [
        moved[..., width_out + j * 2 * head_count : width_out + (j + 1) * 2 * head_count].astype(
            jnp.float32
        )
        for j in range(3)
    ]
    moved_stats = (parts[0] + parts[1]) + parts[2]
    cache_part = (
        moved[..., :width_out],
        moved_stats[..., :head_count],
        moved_stats[..., head_count:],
    )
    attention = merge_parts(cache_part, draft_part, HEAD_SIZE)
    every_row = gather_rows(attention, "blk")
    partial = jnp.dot(every_row, out_weight, preferred_element_type=jnp.float32)
    out_rows = partial.shape[0] // kv_count
    arrived = lax.all_to_all(
        partial.reshape(kv_count, out_rows, partial.shape[1]),
        "kv",
        split_axis=0,
        concat_axis=0,
        tiled=True,
    )
    projected = jnp.sum(arrived, axis=0).astype(jnp.bfloat16)
    positions_here = my_block * block_len + jnp.arange(block_len, dtype=jnp.int32)
    offset = positions_here[None, :] - lengths[:, None]
    written = (offset >= 0) & (offset < accepted_count[:, None])
    slot_match = offset[:, :, None] == jnp.arange(ACC, dtype=jnp.int32)[None, None, :]
    node_ids = jnp.sum(jnp.where(slot_match, accepted_nodes[:, None, :], 0), axis=-1)
    new_cache_keys = place_rows(
        gathered_keys.reshape(requests, TREE_TOKENS, cache_width),
        node_ids,
        written,
        cached_key_vectors,
    )
    new_cache_values = place_rows(
        gathered_values.reshape(requests, TREE_TOKENS, cache_width),
        node_ids,
        written,
        cached_value_vectors,
    )
    return (projected, new_cache_keys, new_cache_values)


def solution(mesh):
    return jax.shard_map(
        on_device,
        mesh=mesh,
        in_specs=(
            P("blk", "kv"),
            P("blk", "kv"),
            P("blk", "kv"),
            P(None, "blk", "kv"),
            P(None, "blk", "kv"),
            P("kv", "blk"),
            P(),
            P(),
            P(),
            P(),
        ),
        out_specs=(P("kv", "blk"), P(None, "blk", "kv"), P(None, "blk", "kv")),
        check_vma=False,
    )
```

```python
import math

import jax
import jax.numpy as jnp
from jax import lax
from jax.sharding import PartitionSpec as P
from jax.experimental import pallas as pl
from jax.experimental.pallas import tpu as pltpu

HEAD_SIZE = 128
TREE_TOKENS = 64
ACC = 8


NEG_FLOOR = -1e30


def ancestors(parent_rows):
    node_ids = jnp.arange(TREE_TOKENS, dtype=jnp.int32)
    parent_link = (
        (parent_rows[:, :, None] == node_ids[None, None, :]) & (node_ids[None, :, None] >= 1)
    ).astype(jnp.float32)
    reachable = jnp.eye(TREE_TOKENS, dtype=jnp.float32)[None] + parent_link
    for doubling in range((TREE_TOKENS - 1).bit_length()):
        reachable = jnp.minimum(
            reachable
            + jnp.einsum("rij,rjk->rik", reachable, reachable, precision=lax.Precision.HIGHEST),
            1.0,
        )
    return reachable


def partial_softmax(query_vectors, key_rows, value_rows, usable, score_scale):
    scores = (
        jnp.einsum(
            "rtkgh,rbpkh->brkgtp", query_vectors, key_rows, preferred_element_type=jnp.float32
        )
        * score_scale
    )
    scores = jnp.where(usable, scores, NEG_FLOOR)
    peak_score = jnp.max(scores, axis=-1)
    weights = jnp.where(usable, jnp.exp(scores - peak_score[..., None]), 0.0)
    weight_sum = jnp.sum(weights, axis=-1)
    weighted = jnp.einsum(
        "brkgtp,rbpkh->brtkgh",
        weights.astype(jnp.bfloat16),
        value_rows,
        preferred_element_type=jnp.float32,
    )
    block_count, req_count, kv_count, query_group_width, row_count = peak_score.shape
    weighted = weighted.reshape(
        block_count, req_count * row_count, kv_count * query_group_width * value_rows.shape[-1]
    )
    peak_score = peak_score.transpose(0, 1, 4, 2, 3).reshape(
        block_count, req_count * row_count, kv_count * query_group_width
    )
    weight_sum = weight_sum.transpose(0, 1, 4, 2, 3).reshape(
        block_count, req_count * row_count, kv_count * query_group_width
    )
    return (weighted, peak_score, weight_sum)


def merge_parts(cache_part, draft_part, head_dim):
    cache_out, cache_peak, cache_sum = cache_part
    draft_out, draft_peak, draft_sum = draft_part
    cache_out = cache_out.astype(jnp.float32)
    overall = jnp.maximum(jnp.max(cache_peak, axis=0), draft_peak[0])
    cache_factor = jnp.exp(cache_peak - overall[None])
    draft_factor = jnp.exp(draft_peak[0] - overall)
    denominator = jnp.sum(cache_factor * cache_sum, axis=0) + draft_factor * draft_sum[0]
    block_count, row_count, head_count = cache_peak.shape
    numerator = jnp.sum(
        cache_factor[..., None] * cache_out.reshape(block_count, row_count, head_count, head_dim),
        axis=0,
    )
    numerator = numerator + draft_factor[..., None] * draft_out[0].reshape(
        row_count, head_count, head_dim
    )
    return (
        (numerator / denominator[..., None])
        .reshape(row_count, head_count * head_dim)
        .astype(jnp.bfloat16)
    )


def place_rows(sources, slot_index, written, cache_rows):
    slot_ids = jnp.arange(sources.shape[1], dtype=jnp.int32)
    selector = ((slot_index[:, :, None] == slot_ids[None, None, :]) & written[:, :, None]).astype(
        jnp.bfloat16
    )
    placed = jnp.einsum(
        "rps,rsc->rpc", selector, sources, preferred_element_type=jnp.float32
    ).astype(jnp.bfloat16)
    return jnp.where(written[:, :, None], placed, cache_rows)


def split_three(x):
    hi = x.astype(jnp.bfloat16)
    rest = x - hi.astype(jnp.float32)
    mid = rest.astype(jnp.bfloat16)
    lo = (rest - mid.astype(jnp.float32)).astype(jnp.bfloat16)
    return hi, mid, lo


def block_attention_kernel(limit_ref, q_ref, k_ref, v_ref, out_ref, stats_ref):
    requests, block_len, _ = k_ref.shape
    rows = out_ref.shape[0] // requests
    heads = stats_ref.shape[1] // 2
    score_scale = 1.0 / math.sqrt(HEAD_SIZE)
    for r in range(requests):
        q = jnp.concatenate(
            [
                q_ref[r * rows : (r + 1) * rows, h * HEAD_SIZE : (h + 1) * HEAD_SIZE]
                for h in range(heads)
            ],
            axis=0,
        )
        scores = (
            lax.dot_general(
                q, k_ref[r], (((1,), (1,)), ((), ())), preferred_element_type=jnp.float32
            )
            * score_scale
        )
        valid = lax.broadcasted_iota(jnp.int32, scores.shape, 1) < limit_ref[r]
        scores = jnp.where(valid, scores, NEG_FLOOR)
        peak = jnp.max(scores, axis=1, keepdims=True)
        weights = jnp.where(valid, jnp.exp(scores - peak), 0.0)
        total = jnp.sum(weights, axis=1, keepdims=True)
        out = jnp.dot(
            weights.astype(jnp.bfloat16), v_ref[r], preferred_element_type=jnp.float32
        ).astype(out_ref.dtype)
        for h in range(heads):
            here = slice(h * rows, (h + 1) * rows)
            out_ref[r * rows : (r + 1) * rows, h * HEAD_SIZE : (h + 1) * HEAD_SIZE] = out[here]
            stats_ref[r * rows : (r + 1) * rows, h : h + 1] = peak[here]
            stats_ref[r * rows : (r + 1) * rows, heads + h : heads + h + 1] = total[here]
    width = heads * HEAD_SIZE
    stats = stats_ref[...]
    for j, part in enumerate(split_three(stats)):
        out_ref[:, width + j * 2 * heads : width + (j + 1) * 2 * heads] = part


def block_attention(limit, every_query, keys, values, width):
    rows = every_query.shape[0]
    heads = width // HEAD_SIZE
    requests, block_len, _ = keys.shape
    vmem = pl.BlockSpec(memory_space=pltpu.VMEM)
    return pl.pallas_call(
        block_attention_kernel,
        out_shape=jax.ShapeDtypeStruct((rows, width + 6 * heads), jnp.bfloat16),
        in_specs=[pl.BlockSpec(memory_space=pltpu.SMEM), vmem, vmem, vmem],
        out_specs=vmem,
        scratch_shapes=[pltpu.VMEM((rows, 2 * heads), jnp.float32)],
        cost_estimate=pl.CostEstimate(
            flops=4 * rows * heads * block_len * HEAD_SIZE,
            transcendentals=rows * heads * block_len,
            bytes_accessed=2 * (rows * width + 2 * requests * block_len * HEAD_SIZE + rows * (width + 6 * heads)),
        ),
    )(limit, every_query, keys, values)


def gather_rows(block, axis_name):
    count = lax.axis_size(axis_name)
    spread = jnp.broadcast_to(block[None], (count,) + block.shape)
    moved = lax.all_to_all(spread, axis_name, split_axis=0, concat_axis=0, tiled=True)
    return moved.reshape((count * block.shape[0],) + block.shape[1:])


def on_device(
    queries,
    draft_token_keys,
    draft_token_values,
    cached_key_vectors,
    cached_value_vectors,
    out_weight,
    lengths,
    parents,
    accepted_nodes,
    accepted_count,
):
    block_count = lax.axis_size("blk")
    kv_count = lax.axis_size("kv")
    my_block = lax.axis_index("blk")
    rows_dev, width_q = queries.shape
    requests = lengths.shape[0]
    cache_width = cached_key_vectors.shape[2]
    kv_local = cache_width // HEAD_SIZE
    query_group_width = width_q // (kv_local * HEAD_SIZE)
    block_len = cached_key_vectors.shape[1]
    score_scale = 1.0 / math.sqrt(HEAD_SIZE)
    leading_row = my_block * rows_dev
    my_request = leading_row // TREE_TOKENS
    node_start = leading_row - my_request * TREE_TOKENS
    local_queries = queries.reshape(1, rows_dev, kv_local, query_group_width, HEAD_SIZE)
    packed = gather_rows(
        jnp.concatenate([queries, draft_token_keys, draft_token_values], axis=1), "blk"
    )
    every_query = packed[:, :width_q]
    gathered_keys = packed[:, width_q : width_q + cache_width]
    gathered_values = packed[:, width_q + cache_width :]
    tree_keys = lax.dynamic_slice_in_dim(
        gathered_keys, my_request * TREE_TOKENS, TREE_TOKENS, 0
    ).reshape(1, 1, TREE_TOKENS, kv_local, HEAD_SIZE)
    tree_values = lax.dynamic_slice_in_dim(
        gathered_values, my_request * TREE_TOKENS, TREE_TOKENS, 0
    ).reshape(1, 1, TREE_TOKENS, kv_local, HEAD_SIZE)
    reachable = ancestors(lax.dynamic_slice_in_dim(parents, my_request, 1, 0))
    own_reach = lax.dynamic_slice_in_dim(reachable, node_start, rows_dev, 1)
    draft_usable = (own_reach > 0.5)[None, :, None, None, :, :]
    draft_part = partial_softmax(local_queries, tree_keys, tree_values, draft_usable, score_scale)
    limit = lengths - my_block * block_len
    packed_out = block_attention(
        limit, packed, cached_key_vectors, cached_value_vectors, width_q
    )
    head_count = width_q // HEAD_SIZE
    width_out = width_q
    moved = lax.all_to_all(packed_out, "blk", split_axis=0, concat_axis=0, tiled=True)
    moved = moved.reshape(block_count, rows_dev, -1)
    parts = [
        moved[..., width_out + j * 2 * head_count : width_out + (j + 1) * 2 * head_count].astype(
            jnp.float32
        )
        for j in range(3)
    ]
    moved_stats = (parts[0] + parts[1]) + parts[2]
    cache_part = (
        moved[..., :width_out],
        moved_stats[..., :head_count],
        moved_stats[..., head_count:],
    )
    attention = merge_parts(cache_part, draft_part, HEAD_SIZE)
    every_row = gather_rows(attention, "blk")
    partial = jnp.dot(every_row, out_weight, preferred_element_type=jnp.float32)
    out_rows = partial.shape[0] // kv_count
    arrived = lax.all_to_all(
        partial.reshape(kv_count, out_rows, partial.shape[1]),
        "kv",
        split_axis=0,
        concat_axis=0,
        tiled=True,
    )
    projected = jnp.sum(arrived, axis=0).astype(jnp.bfloat16)
    positions_here = my_block * block_len + jnp.arange(block_len, dtype=jnp.int32)
    offset = positions_here[None, :] - lengths[:, None]
    written = (offset >= 0) & (offset < accepted_count[:, None])
    slot_match = offset[:, :, None] == jnp.arange(ACC, dtype=jnp.int32)[None, None, :]
    node_ids = jnp.sum(jnp.where(slot_match, accepted_nodes[:, None, :], 0), axis=-1)
    new_cache_keys = place_rows(
        gathered_keys.reshape(requests, TREE_TOKENS, cache_width),
        node_ids,
        written,
        cached_key_vectors,
    )
    new_cache_values = place_rows(
        gathered_values.reshape(requests, TREE_TOKENS, cache_width),
        node_ids,
        written,
        cached_value_vectors,
    )
    return (projected, new_cache_keys, new_cache_values)


def solution(mesh):
    return jax.shard_map(
        on_device,
        mesh=mesh,
        in_specs=(
            P("blk", "kv"),
            P("blk", "kv"),
            P("blk", "kv"),
            P(None, "blk", "kv"),
            P(None, "blk", "kv"),
            P("kv", "blk"),
            P(),
            P(),
            P(),
            P(),
        ),
        out_specs=(P("kv", "blk"), P(None, "blk", "kv"), P(None, "blk", "kv")),
        check_vma=False,
    )
```

```python
import math

import jax
import jax.numpy as jnp
from jax import lax
from jax.sharding import Mesh, PartitionSpec as P
from jax.experimental import pallas as pl
from jax.experimental.pallas import tpu as pltpu

HEAD_SIZE = 128
TREE_TOKENS = 64
ACC = 8


NEG_FLOOR = -1e30


def ancestors(parent_rows):
    node_ids = jnp.arange(TREE_TOKENS, dtype=jnp.int32)
    parent_link = (
        (parent_rows[:, :, None] == node_ids[None, None, :]) & (node_ids[None, :, None] >= 1)
    ).astype(jnp.float32)
    reachable = jnp.eye(TREE_TOKENS, dtype=jnp.float32)[None] + parent_link
    for doubling in range((TREE_TOKENS - 1).bit_length()):
        reachable = jnp.minimum(
            reachable
            + jnp.einsum("rij,rjk->rik", reachable, reachable, precision=lax.Precision.HIGHEST),
            1.0,
        )
    return reachable


def partial_softmax(query_vectors, key_rows, value_rows, usable, score_scale):
    scores = (
        jnp.einsum(
            "rtkgh,rbpkh->brkgtp", query_vectors, key_rows, preferred_element_type=jnp.float32
        )
        * score_scale
    )
    scores = jnp.where(usable, scores, NEG_FLOOR)
    peak_score = jnp.max(scores, axis=-1)
    weights = jnp.where(usable, jnp.exp(scores - peak_score[..., None]), 0.0)
    weight_sum = jnp.sum(weights, axis=-1)
    weighted = jnp.einsum(
        "brkgtp,rbpkh->brtkgh",
        weights.astype(jnp.bfloat16),
        value_rows,
        preferred_element_type=jnp.float32,
    )
    block_count, req_count, kv_count, query_group_width, row_count = peak_score.shape
    weighted = weighted.reshape(
        block_count, req_count * row_count, kv_count * query_group_width * value_rows.shape[-1]
    )
    peak_score = peak_score.transpose(0, 1, 4, 2, 3).reshape(
        block_count, req_count * row_count, kv_count * query_group_width
    )
    weight_sum = weight_sum.transpose(0, 1, 4, 2, 3).reshape(
        block_count, req_count * row_count, kv_count * query_group_width
    )
    return (weighted, peak_score, weight_sum)


def merge_parts(cache_part, draft_part, head_dim):
    cache_out, cache_peak, cache_sum = cache_part
    draft_out, draft_peak, draft_sum = draft_part
    cache_out = cache_out.astype(jnp.float32)
    overall = jnp.maximum(jnp.max(cache_peak, axis=0), draft_peak[0])
    cache_factor = jnp.exp(cache_peak - overall[None])
    draft_factor = jnp.exp(draft_peak[0] - overall)
    denominator = jnp.sum(cache_factor * cache_sum, axis=0) + draft_factor * draft_sum[0]
    block_count, row_count, head_count = cache_peak.shape
    numerator = jnp.sum(
        cache_factor[..., None] * cache_out.reshape(block_count, row_count, head_count, head_dim),
        axis=0,
    )
    numerator = numerator + draft_factor[..., None] * draft_out[0].reshape(
        row_count, head_count, head_dim
    )
    return (
        (numerator / denominator[..., None])
        .reshape(row_count, head_count * head_dim)
        .astype(jnp.bfloat16)
    )


def place_rows(sources, slot_index, written, cache_rows):
    slot_ids = jnp.arange(sources.shape[1], dtype=jnp.int32)
    selector = ((slot_index[:, :, None] == slot_ids[None, None, :]) & written[:, :, None]).astype(
        jnp.bfloat16
    )
    placed = jnp.einsum(
        "rps,rsc->rpc", selector, sources, preferred_element_type=jnp.float32
    ).astype(jnp.bfloat16)
    return jnp.where(written[:, :, None], placed, cache_rows)


def split_three(x):
    hi = x.astype(jnp.bfloat16)
    rest = x - hi.astype(jnp.float32)
    mid = rest.astype(jnp.bfloat16)
    lo = (rest - mid.astype(jnp.float32)).astype(jnp.bfloat16)
    return hi, mid, lo


def block_attention_kernel(limit_ref, q_ref, kv_ref, out_ref, stats_ref):
    blocks, block_len, _ = kv_ref.shape
    rows = out_ref.shape[0]
    heads = stats_ref.shape[1] // 2
    score_scale = 1.0 / math.sqrt(HEAD_SIZE)
    q = jnp.concatenate(
        [q_ref[:, h * HEAD_SIZE : (h + 1) * HEAD_SIZE] for h in range(heads)], axis=0
    )
    scores = []
    valids = []
    for b in range(blocks):
        s = (
            lax.dot_general(
                q,
                kv_ref[b, :, :HEAD_SIZE],
                (((1,), (1,)), ((), ())),
                preferred_element_type=jnp.float32,
            )
            * score_scale
        )
        valid = lax.broadcasted_iota(jnp.int32, s.shape, 1) < limit_ref[b]
        scores.append(jnp.where(valid, s, NEG_FLOOR))
        valids.append(valid)
    peak = jnp.max(scores[0], axis=1, keepdims=True)
    for s in scores[1:]:
        peak = jnp.maximum(peak, jnp.max(s, axis=1, keepdims=True))
    total = jnp.zeros_like(peak)
    out = jnp.zeros((q.shape[0], HEAD_SIZE), jnp.float32)
    for b in range(blocks):
        weights = jnp.where(valids[b], jnp.exp(scores[b] - peak), 0.0)
        total = total + jnp.sum(weights, axis=1, keepdims=True)
        out = out + jnp.dot(
            weights.astype(jnp.bfloat16),
            kv_ref[b, :, HEAD_SIZE:],
            preferred_element_type=jnp.float32,
        )
    out = out.astype(out_ref.dtype)
    for h in range(heads):
        here = slice(h * rows, (h + 1) * rows)
        out_ref[:, h * HEAD_SIZE : (h + 1) * HEAD_SIZE] = out[here]
        stats_ref[:, h : h + 1] = peak[here]
        stats_ref[:, heads + h : heads + h + 1] = total[here]
    width = heads * HEAD_SIZE
    stats = stats_ref[...]
    for j, part in enumerate(split_three(stats)):
        out_ref[:, width + j * 2 * heads : width + (j + 1) * 2 * heads] = part


def block_attention(limit, group_rows, blocks_kv, width):
    rows = group_rows.shape[0]
    heads = width // HEAD_SIZE
    blocks, block_len, _ = blocks_kv.shape
    vmem = pl.BlockSpec(memory_space=pltpu.VMEM)
    return pl.pallas_call(
        block_attention_kernel,
        out_shape=jax.ShapeDtypeStruct((rows, width + 6 * heads), jnp.bfloat16),
        in_specs=[pl.BlockSpec(memory_space=pltpu.SMEM), vmem, vmem],
        out_specs=vmem,
        scratch_shapes=[pltpu.VMEM((rows, 2 * heads), jnp.float32)],
        cost_estimate=pl.CostEstimate(
            flops=4 * rows * heads * blocks * block_len * HEAD_SIZE,
            transcendentals=rows * heads * blocks * block_len,
            bytes_accessed=2 * (rows * width + 2 * blocks * block_len * HEAD_SIZE + rows * (width + 6 * heads)),
        ),
    )(limit, group_rows, blocks_kv)


def gather_rows(block, axis_name):
    count = lax.axis_size(axis_name)
    spread = jnp.broadcast_to(block[None], (count,) + block.shape)
    moved = lax.all_to_all(spread, axis_name, split_axis=0, concat_axis=0, tiled=True)
    return moved.reshape((count * block.shape[0],) + block.shape[1:])


def on_device(
    queries,
    draft_token_keys,
    draft_token_values,
    cached_key_vectors,
    cached_value_vectors,
    out_weight,
    lengths,
    parents,
    accepted_nodes,
    accepted_count,
):
    blk = ("bx", "bz")
    kv_count = lax.axis_size("kv")
    ring = lax.axis_size("bz")
    my_block = lax.axis_index(blk)
    my_x = lax.axis_index("bx")
    my_z = lax.axis_index("bz")
    rows_dev, width_q = queries.shape
    requests = lengths.shape[0]
    cache_width = cached_key_vectors.shape[2]
    kv_local = cache_width // HEAD_SIZE
    query_group_width = width_q // (kv_local * HEAD_SIZE)
    block_len = cached_key_vectors.shape[1]
    score_scale = 1.0 / math.sqrt(HEAD_SIZE)
    my_request = my_x
    node_start = my_z * rows_dev
    local_queries = queries.reshape(1, rows_dev, kv_local, query_group_width, HEAD_SIZE)
    own_draft = jnp.concatenate([draft_token_keys, draft_token_values], axis=1)
    group_rows = gather_rows(jnp.concatenate([queries, own_draft], axis=1), "bz")
    blocks_kv = lax.all_to_all(
        jnp.concatenate([cached_key_vectors, cached_value_vectors], axis=2),
        "bx",
        split_axis=0,
        concat_axis=0,
        tiled=True,
    )
    tree_keys = group_rows[:, width_q : width_q + cache_width].reshape(
        1, 1, TREE_TOKENS, kv_local, HEAD_SIZE
    )
    tree_values = group_rows[:, width_q + cache_width :].reshape(
        1, 1, TREE_TOKENS, kv_local, HEAD_SIZE
    )
    reachable = ancestors(lax.dynamic_slice_in_dim(parents, my_request, 1, 0))
    own_reach = lax.dynamic_slice_in_dim(reachable, node_start, rows_dev, 1)
    draft_usable = (own_reach > 0.5)[None, :, None, None, :, :]
    draft_part = partial_softmax(local_queries, tree_keys, tree_values, draft_usable, score_scale)
    source_blocks = jnp.arange(blocks_kv.shape[0], dtype=jnp.int32) * ring + my_z
    limit = lengths[my_request] - source_blocks * block_len
    packed_out = block_attention(limit, group_rows, blocks_kv, width_q)
    head_count = width_q // HEAD_SIZE
    width_out = width_q
    moved = lax.all_to_all(
        packed_out.reshape(ring, rows_dev, -1), "bz", split_axis=0, concat_axis=0, tiled=True
    )
    parts = [
        moved[..., width_out + j * 2 * head_count : width_out + (j + 1) * 2 * head_count].astype(
            jnp.float32
        )
        for j in range(3)
    ]
    moved_stats = (parts[0] + parts[1]) + parts[2]
    cache_part = (
        moved[..., :width_out],
        moved_stats[..., :head_count],
        moved_stats[..., head_count:],
    )
    attention = merge_parts(cache_part, draft_part, HEAD_SIZE)
    every_row = gather_rows(jnp.concatenate([attention, own_draft], axis=1), blk)
    gathered_keys = every_row[:, width_q : width_q + cache_width]
    gathered_values = every_row[:, width_q + cache_width :]
    partial = jnp.dot(every_row[:, :width_q], out_weight, preferred_element_type=jnp.float32)
    out_rows = partial.shape[0] // kv_count
    arrived = lax.all_to_all(
        partial.reshape(kv_count, out_rows, partial.shape[1]),
        "kv",
        split_axis=0,
        concat_axis=0,
        tiled=True,
    )
    projected = jnp.sum(arrived, axis=0).astype(jnp.bfloat16)
    positions_here = my_block * block_len + jnp.arange(block_len, dtype=jnp.int32)
    offset = positions_here[None, :] - lengths[:, None]
    written = (offset >= 0) & (offset < accepted_count[:, None])
    slot_match = offset[:, :, None] == jnp.arange(ACC, dtype=jnp.int32)[None, None, :]
    node_ids = jnp.sum(jnp.where(slot_match, accepted_nodes[:, None, :], 0), axis=-1)
    new_cache_keys = place_rows(
        gathered_keys.reshape(requests, TREE_TOKENS, cache_width),
        node_ids,
        written,
        cached_key_vectors,
    )
    new_cache_values = place_rows(
        gathered_values.reshape(requests, TREE_TOKENS, cache_width),
        node_ids,
        written,
        cached_value_vectors,
    )
    return (projected, new_cache_keys, new_cache_values)


def solution(mesh):
    kv_size, blk_size = mesh.devices.shape
    requests = 4
    ring = blk_size // requests
    grid_mesh = Mesh(mesh.devices.reshape(kv_size, requests, ring), ("kv", "bx", "bz"))
    blk = ("bx", "bz")
    return jax.shard_map(
        on_device,
        mesh=grid_mesh,
        in_specs=(
            P(blk, "kv"),
            P(blk, "kv"),
            P(blk, "kv"),
            P(None, blk, "kv"),
            P(None, blk, "kv"),
            P("kv", blk),
            P(),
            P(),
            P(),
            P(),
        ),
        out_specs=(P("kv", blk), P(None, blk, "kv"), P(None, blk, "kv")),
        check_vma=False,
    )
```

```python
import math

import jax
import jax.numpy as jnp
from jax import lax
from jax.sharding import Mesh, PartitionSpec as P
from jax.experimental import pallas as pl
from jax.experimental.pallas import tpu as pltpu

HEAD_SIZE = 128
TREE_TOKENS = 64
ACC = 8


NEG_FLOOR = -1e30


def ancestors(parent_rows):
    node_ids = jnp.arange(TREE_TOKENS, dtype=jnp.int32)
    parent_link = (
        (parent_rows[:, :, None] == node_ids[None, None, :]) & (node_ids[None, :, None] >= 1)
    ).astype(jnp.float32)
    reachable = jnp.eye(TREE_TOKENS, dtype=jnp.float32)[None] + parent_link
    for doubling in range((TREE_TOKENS - 1).bit_length()):
        reachable = jnp.minimum(
            reachable
            + jnp.einsum("rij,rjk->rik", reachable, reachable, precision=lax.Precision.HIGHEST),
            1.0,
        )
    return reachable


def partial_softmax(query_vectors, key_rows, value_rows, usable, score_scale):
    scores = (
        jnp.einsum(
            "rtkgh,rbpkh->brkgtp", query_vectors, key_rows, preferred_element_type=jnp.float32
        )
        * score_scale
    )
    scores = jnp.where(usable, scores, NEG_FLOOR)
    peak_score = jnp.max(scores, axis=-1)
    weights = jnp.where(usable, jnp.exp(scores - peak_score[..., None]), 0.0)
    weight_sum = jnp.sum(weights, axis=-1)
    weighted = jnp.einsum(
        "brkgtp,rbpkh->brtkgh",
        weights.astype(jnp.bfloat16),
        value_rows,
        preferred_element_type=jnp.float32,
    )
    block_count, req_count, kv_count, query_group_width, row_count = peak_score.shape
    weighted = weighted.reshape(
        block_count, req_count * row_count, kv_count * query_group_width * value_rows.shape[-1]
    )
    peak_score = peak_score.transpose(0, 1, 4, 2, 3).reshape(
        block_count, req_count * row_count, kv_count * query_group_width
    )
    weight_sum = weight_sum.transpose(0, 1, 4, 2, 3).reshape(
        block_count, req_count * row_count, kv_count * query_group_width
    )
    return (weighted, peak_score, weight_sum)


def merge_parts(cache_part, draft_part, head_dim):
    cache_out, cache_peak, cache_sum = cache_part
    draft_out, draft_peak, draft_sum = draft_part
    cache_out = cache_out.astype(jnp.float32)
    overall = jnp.maximum(jnp.max(cache_peak, axis=0), draft_peak[0])
    cache_factor = jnp.exp(cache_peak - overall[None])
    draft_factor = jnp.exp(draft_peak[0] - overall)
    denominator = jnp.sum(cache_factor * cache_sum, axis=0) + draft_factor * draft_sum[0]
    block_count, row_count, head_count = cache_peak.shape
    numerator = jnp.sum(
        cache_factor[..., None] * cache_out.reshape(block_count, row_count, head_count, head_dim),
        axis=0,
    )
    numerator = numerator + draft_factor[..., None] * draft_out[0].reshape(
        row_count, head_count, head_dim
    )
    return (
        (numerator / denominator[..., None])
        .reshape(row_count, head_count * head_dim)
        .astype(jnp.bfloat16)
    )


def place_rows(sources, slot_index, written, cache_rows):
    slot_ids = jnp.arange(sources.shape[1], dtype=jnp.int32)
    selector = ((slot_index[:, :, None] == slot_ids[None, None, :]) & written[:, :, None]).astype(
        jnp.bfloat16
    )
    placed = jnp.einsum(
        "rps,rsc->rpc", selector, sources, preferred_element_type=jnp.float32
    ).astype(jnp.bfloat16)
    return jnp.where(written[:, :, None], placed, cache_rows)


def split_three(x):
    hi = x.astype(jnp.bfloat16)
    rest = x - hi.astype(jnp.float32)
    mid = rest.astype(jnp.bfloat16)
    lo = (rest - mid.astype(jnp.float32)).astype(jnp.bfloat16)
    return hi, mid, lo


def block_attention_kernel(limit_ref, q_ref, kv_ref, out_ref, stats_ref):
    blocks, block_len, _ = kv_ref.shape
    rows = out_ref.shape[0]
    heads = stats_ref.shape[1] // 2
    score_scale = 1.0 / math.sqrt(HEAD_SIZE)
    q = jnp.concatenate(
        [q_ref[:, h * HEAD_SIZE : (h + 1) * HEAD_SIZE] for h in range(heads)], axis=0
    )
    scores = []
    valids = []
    for b in range(blocks):
        s = (
            lax.dot_general(
                q,
                kv_ref[b, :, :HEAD_SIZE],
                (((1,), (1,)), ((), ())),
                preferred_element_type=jnp.float32,
            )
            * score_scale
        )
        valid = lax.broadcasted_iota(jnp.int32, s.shape, 1) < limit_ref[b]
        scores.append(jnp.where(valid, s, NEG_FLOOR))
        valids.append(valid)
    peak = jnp.max(scores[0], axis=1, keepdims=True)
    for s in scores[1:]:
        peak = jnp.maximum(peak, jnp.max(s, axis=1, keepdims=True))
    total = jnp.zeros_like(peak)
    out = jnp.zeros((q.shape[0], HEAD_SIZE), jnp.float32)
    for b in range(blocks):
        weights = jnp.where(valids[b], jnp.exp(scores[b] - peak), 0.0)
        total = total + jnp.sum(weights, axis=1, keepdims=True)
        out = out + jnp.dot(
            weights.astype(jnp.bfloat16),
            kv_ref[b, :, HEAD_SIZE:],
            preferred_element_type=jnp.float32,
        )
    out = out.astype(out_ref.dtype)
    for h in range(heads):
        here = slice(h * rows, (h + 1) * rows)
        out_ref[:, h * HEAD_SIZE : (h + 1) * HEAD_SIZE] = out[here]
        stats_ref[:, h : h + 1] = peak[here]
        stats_ref[:, heads + h : heads + h + 1] = total[here]
    width = heads * HEAD_SIZE
    stats = stats_ref[...]
    for j, part in enumerate(split_three(stats)):
        out_ref[:, width + j * 2 * heads : width + (j + 1) * 2 * heads] = part


def block_attention(limit, group_rows, blocks_kv, width):
    rows = group_rows.shape[0]
    heads = width // HEAD_SIZE
    blocks, block_len, _ = blocks_kv.shape
    vmem = pl.BlockSpec(memory_space=pltpu.VMEM)
    return pl.pallas_call(
        block_attention_kernel,
        out_shape=jax.ShapeDtypeStruct((rows, width + 6 * heads), jnp.bfloat16),
        in_specs=[pl.BlockSpec(memory_space=pltpu.SMEM), vmem, vmem],
        out_specs=vmem,
        scratch_shapes=[pltpu.VMEM((rows, 2 * heads), jnp.float32)],
        cost_estimate=pl.CostEstimate(
            flops=4 * rows * heads * blocks * block_len * HEAD_SIZE,
            transcendentals=rows * heads * blocks * block_len,
            bytes_accessed=2 * (rows * width + 2 * blocks * block_len * HEAD_SIZE + rows * (width + 6 * heads)),
        ),
    )(limit, group_rows, blocks_kv)


def gather_rows(block, axis_name):
    count = lax.axis_size(axis_name)
    spread = jnp.broadcast_to(block[None], (count,) + block.shape)
    moved = lax.all_to_all(spread, axis_name, split_axis=0, concat_axis=0, tiled=True)
    return moved.reshape((count * block.shape[0],) + block.shape[1:])


def on_device(
    queries,
    draft_token_keys,
    draft_token_values,
    cached_key_vectors,
    cached_value_vectors,
    out_weight,
    lengths,
    parents,
    accepted_nodes,
    accepted_count,
):
    blk = ("bx", "bz")
    kv_count = lax.axis_size("kv")
    ring = lax.axis_size("bz")
    my_block = lax.axis_index(blk)
    my_x = lax.axis_index("bx")
    my_z = lax.axis_index("bz")
    rows_dev, width_q = queries.shape
    requests = lengths.shape[0]
    cache_width = cached_key_vectors.shape[2]
    kv_local = cache_width // HEAD_SIZE
    query_group_width = width_q // (kv_local * HEAD_SIZE)
    block_len = cached_key_vectors.shape[1]
    score_scale = 1.0 / math.sqrt(HEAD_SIZE)
    my_request = my_x
    node_start = my_z * rows_dev
    local_queries = queries.reshape(1, rows_dev, kv_local, query_group_width, HEAD_SIZE)
    own_draft = jnp.concatenate([draft_token_keys, draft_token_values], axis=1)
    group_rows = gather_rows(jnp.concatenate([queries, own_draft], axis=1), "bz")
    cache_pair = jnp.concatenate([cached_key_vectors, cached_value_vectors], axis=2)
    group_rows, cache_pair = lax.optimization_barrier((group_rows, cache_pair))
    blocks_kv = lax.all_to_all(
        cache_pair,
        "bx",
        split_axis=0,
        concat_axis=0,
        tiled=True,
    )
    tree_keys = group_rows[:, width_q : width_q + cache_width].reshape(
        1, 1, TREE_TOKENS, kv_local, HEAD_SIZE
    )
    tree_values = group_rows[:, width_q + cache_width :].reshape(
        1, 1, TREE_TOKENS, kv_local, HEAD_SIZE
    )
    reachable = ancestors(lax.dynamic_slice_in_dim(parents, my_request, 1, 0))
    own_reach = lax.dynamic_slice_in_dim(reachable, node_start, rows_dev, 1)
    draft_usable = (own_reach > 0.5)[None, :, None, None, :, :]
    draft_part = partial_softmax(local_queries, tree_keys, tree_values, draft_usable, score_scale)
    source_blocks = jnp.arange(blocks_kv.shape[0], dtype=jnp.int32) * ring + my_z
    limit = lengths[my_request] - source_blocks * block_len
    packed_out = block_attention(limit, group_rows, blocks_kv, width_q)
    head_count = width_q // HEAD_SIZE
    width_out = width_q
    moved = lax.all_to_all(
        packed_out.reshape(ring, rows_dev, -1), "bz", split_axis=0, concat_axis=0, tiled=True
    )
    parts = [
        moved[..., width_out + j * 2 * head_count : width_out + (j + 1) * 2 * head_count].astype(
            jnp.float32
        )
        for j in range(3)
    ]
    moved_stats = (parts[0] + parts[1]) + parts[2]
    cache_part = (
        moved[..., :width_out],
        moved_stats[..., :head_count],
        moved_stats[..., head_count:],
    )
    attention = merge_parts(cache_part, draft_part, HEAD_SIZE)
    every_row = gather_rows(jnp.concatenate([attention, own_draft], axis=1), blk)
    gathered_keys = every_row[:, width_q : width_q + cache_width]
    gathered_values = every_row[:, width_q + cache_width :]
    partial = jnp.dot(every_row[:, :width_q], out_weight, preferred_element_type=jnp.float32)
    out_rows = partial.shape[0] // kv_count
    arrived = lax.all_to_all(
        partial.reshape(kv_count, out_rows, partial.shape[1]),
        "kv",
        split_axis=0,
        concat_axis=0,
        tiled=True,
    )
    projected = jnp.sum(arrived, axis=0).astype(jnp.bfloat16)
    positions_here = my_block * block_len + jnp.arange(block_len, dtype=jnp.int32)
    offset = positions_here[None, :] - lengths[:, None]
    written = (offset >= 0) & (offset < accepted_count[:, None])
    slot_match = offset[:, :, None] == jnp.arange(ACC, dtype=jnp.int32)[None, None, :]
    node_ids = jnp.sum(jnp.where(slot_match, accepted_nodes[:, None, :], 0), axis=-1)
    new_cache_keys = place_rows(
        gathered_keys.reshape(requests, TREE_TOKENS, cache_width),
        node_ids,
        written,
        cached_key_vectors,
    )
    new_cache_values = place_rows(
        gathered_values.reshape(requests, TREE_TOKENS, cache_width),
        node_ids,
        written,
        cached_value_vectors,
    )
    return (projected, new_cache_keys, new_cache_values)


def solution(mesh):
    kv_size, blk_size = mesh.devices.shape
    requests = 4
    ring = blk_size // requests
    grid_mesh = Mesh(mesh.devices.reshape(kv_size, requests, ring), ("kv", "bx", "bz"))
    blk = ("bx", "bz")
    return jax.shard_map(
        on_device,
        mesh=grid_mesh,
        in_specs=(
            P(blk, "kv"),
            P(blk, "kv"),
            P(blk, "kv"),
            P(None, blk, "kv"),
            P(None, blk, "kv"),
            P("kv", blk),
            P(),
            P(),
            P(),
            P(),
        ),
        out_specs=(P("kv", blk), P(None, blk, "kv"), P(None, blk, "kv")),
        check_vma=False,
    )
```

```python
import functools
import math

import jax
import jax.numpy as jnp
from jax import lax
from jax.sharding import Mesh, PartitionSpec as P
from jax.experimental import pallas as pl
from jax.experimental.pallas import tpu as pltpu

HEAD_SIZE = 128
TREE_TOKENS = 64
ACC = 8


NEG_FLOOR = -1e30


def ancestors(parent_rows):
    node_ids = jnp.arange(TREE_TOKENS, dtype=jnp.int32)
    parent_link = (
        (parent_rows[:, :, None] == node_ids[None, None, :]) & (node_ids[None, :, None] >= 1)
    ).astype(jnp.float32)
    reachable = jnp.eye(TREE_TOKENS, dtype=jnp.float32)[None] + parent_link
    for doubling in range((TREE_TOKENS - 1).bit_length()):
        reachable = jnp.minimum(
            reachable
            + jnp.einsum("rij,rjk->rik", reachable, reachable, precision=lax.Precision.HIGHEST),
            1.0,
        )
    return reachable


def partial_softmax(query_vectors, key_rows, value_rows, usable, score_scale):
    scores = (
        jnp.einsum(
            "rtkgh,rbpkh->brkgtp", query_vectors, key_rows, preferred_element_type=jnp.float32
        )
        * score_scale
    )
    scores = jnp.where(usable, scores, NEG_FLOOR)
    peak_score = jnp.max(scores, axis=-1)
    weights = jnp.where(usable, jnp.exp(scores - peak_score[..., None]), 0.0)
    weight_sum = jnp.sum(weights, axis=-1)
    weighted = jnp.einsum(
        "brkgtp,rbpkh->brtkgh",
        weights.astype(jnp.bfloat16),
        value_rows,
        preferred_element_type=jnp.float32,
    )
    block_count, req_count, kv_count, query_group_width, row_count = peak_score.shape
    weighted = weighted.reshape(
        block_count, req_count * row_count, kv_count * query_group_width * value_rows.shape[-1]
    )
    peak_score = peak_score.transpose(0, 1, 4, 2, 3).reshape(
        block_count, req_count * row_count, kv_count * query_group_width
    )
    weight_sum = weight_sum.transpose(0, 1, 4, 2, 3).reshape(
        block_count, req_count * row_count, kv_count * query_group_width
    )
    return (weighted, peak_score, weight_sum)


def merge_parts(cache_part, draft_part, head_dim):
    cache_out, cache_peak, cache_sum = cache_part
    draft_out, draft_peak, draft_sum = draft_part
    cache_out = cache_out.astype(jnp.float32)
    overall = jnp.maximum(jnp.max(cache_peak, axis=0), draft_peak[0])
    cache_factor = jnp.exp(cache_peak - overall[None])
    draft_factor = jnp.exp(draft_peak[0] - overall)
    denominator = jnp.sum(cache_factor * cache_sum, axis=0) + draft_factor * draft_sum[0]
    block_count, row_count, head_count = cache_peak.shape
    numerator = jnp.sum(
        cache_factor[..., None] * cache_out.reshape(block_count, row_count, head_count, head_dim),
        axis=0,
    )
    numerator = numerator + draft_factor[..., None] * draft_out[0].reshape(
        row_count, head_count, head_dim
    )
    return (
        (numerator / denominator[..., None])
        .reshape(row_count, head_count * head_dim)
        .astype(jnp.bfloat16)
    )


def place_rows(sources, slot_index, written, cache_rows):
    slot_ids = jnp.arange(sources.shape[1], dtype=jnp.int32)
    selector = ((slot_index[:, :, None] == slot_ids[None, None, :]) & written[:, :, None]).astype(
        jnp.bfloat16
    )
    placed = jnp.einsum(
        "rps,rsc->rpc", selector, sources, preferred_element_type=jnp.float32
    ).astype(jnp.bfloat16)
    return jnp.where(written[:, :, None], placed, cache_rows)


def split_three(x):
    hi = x.astype(jnp.bfloat16)
    rest = x - hi.astype(jnp.float32)
    mid = rest.astype(jnp.bfloat16)
    lo = (rest - mid.astype(jnp.float32)).astype(jnp.bfloat16)
    return hi, mid, lo


def block_attention_kernel(block_len, limit_ref, q_ref, kv_ref, out_ref, stats_ref):
    blocks = kv_ref.shape[0]
    rows = out_ref.shape[0]
    heads = stats_ref.shape[1] // 2
    score_scale = 1.0 / math.sqrt(HEAD_SIZE)
    q = jnp.concatenate(
        [q_ref[:, h * HEAD_SIZE : (h + 1) * HEAD_SIZE] for h in range(heads)], axis=0
    )
    scores = []
    valids = []
    for b in range(blocks):
        s = (
            lax.dot_general(
                q,
                kv_ref[b, :block_len, :HEAD_SIZE],
                (((1,), (1,)), ((), ())),
                preferred_element_type=jnp.float32,
            )
            * score_scale
        )
        valid = lax.broadcasted_iota(jnp.int32, s.shape, 1) < limit_ref[b]
        scores.append(jnp.where(valid, s, NEG_FLOOR))
        valids.append(valid)
    peak = jnp.max(scores[0], axis=1, keepdims=True)
    for s in scores[1:]:
        peak = jnp.maximum(peak, jnp.max(s, axis=1, keepdims=True))
    total = jnp.zeros_like(peak)
    out = jnp.zeros((q.shape[0], HEAD_SIZE), jnp.float32)
    for b in range(blocks):
        weights = jnp.where(valids[b], jnp.exp(scores[b] - peak), 0.0)
        total = total + jnp.sum(weights, axis=1, keepdims=True)
        out = out + jnp.dot(
            weights.astype(jnp.bfloat16),
            kv_ref[b, :block_len, HEAD_SIZE:],
            preferred_element_type=jnp.float32,
        )
    out = out.astype(out_ref.dtype)
    for h in range(heads):
        here = slice(h * rows, (h + 1) * rows)
        out_ref[:, h * HEAD_SIZE : (h + 1) * HEAD_SIZE] = out[here]
        stats_ref[:, h : h + 1] = peak[here]
        stats_ref[:, heads + h : heads + h + 1] = total[here]
    width = heads * HEAD_SIZE
    stats = stats_ref[...]
    for j, part in enumerate(split_three(stats)):
        out_ref[:, width + j * 2 * heads : width + (j + 1) * 2 * heads] = part


def block_attention(limit, group_rows, blocks_kv, width, block_len):
    rows = group_rows.shape[0]
    heads = width // HEAD_SIZE
    blocks = blocks_kv.shape[0]
    vmem = pl.BlockSpec(memory_space=pltpu.VMEM)
    return pl.pallas_call(
        functools.partial(block_attention_kernel, block_len),
        out_shape=jax.ShapeDtypeStruct((rows, width + 6 * heads), jnp.bfloat16),
        in_specs=[pl.BlockSpec(memory_space=pltpu.SMEM), vmem, vmem],
        out_specs=vmem,
        scratch_shapes=[pltpu.VMEM((rows, 2 * heads), jnp.float32)],
        cost_estimate=pl.CostEstimate(
            flops=4 * rows * heads * blocks * block_len * HEAD_SIZE,
            transcendentals=rows * heads * blocks * block_len,
            bytes_accessed=2 * (rows * width + 2 * blocks * block_len * HEAD_SIZE + rows * (width + 6 * heads)),
        ),
    )(limit, group_rows, blocks_kv)


def gather_rows(block, axis_name):
    count = lax.axis_size(axis_name)
    spread = jnp.broadcast_to(block[None], (count,) + block.shape)
    moved = lax.all_to_all(spread, axis_name, split_axis=0, concat_axis=0, tiled=True)
    return moved.reshape((count * block.shape[0],) + block.shape[1:])


def on_device(
    queries,
    draft_token_keys,
    draft_token_values,
    cached_key_vectors,
    cached_value_vectors,
    out_weight,
    lengths,
    parents,
    accepted_nodes,
    accepted_count,
):
    blk = ("bx", "bz")
    kv_count = lax.axis_size("kv")
    ring = lax.axis_size("bz")
    my_block = lax.axis_index(blk)
    my_x = lax.axis_index("bx")
    my_z = lax.axis_index("bz")
    rows_dev, width_q = queries.shape
    requests = lengths.shape[0]
    cache_width = cached_key_vectors.shape[2]
    kv_local = cache_width // HEAD_SIZE
    query_group_width = width_q // (kv_local * HEAD_SIZE)
    block_len = cached_key_vectors.shape[1]
    score_scale = 1.0 / math.sqrt(HEAD_SIZE)
    my_request = my_x
    node_start = my_z * rows_dev
    local_queries = queries.reshape(1, rows_dev, kv_local, query_group_width, HEAD_SIZE)
    own_draft = jnp.concatenate([draft_token_keys, draft_token_values], axis=1)
    group_rows = gather_rows(jnp.concatenate([queries, own_draft], axis=1), "bz")
    cache_pair = jnp.concatenate([cached_key_vectors, cached_value_vectors], axis=2)
    path_pick = (
        accepted_nodes[my_request][:, None] == jnp.arange(TREE_TOKENS, dtype=jnp.int32)[None, :]
    ).astype(jnp.bfloat16)
    path_rows = jnp.dot(
        path_pick, group_rows[:, width_q:], preferred_element_type=jnp.float32
    ).astype(jnp.bfloat16)
    outgoing = jnp.concatenate(
        [cache_pair, jnp.broadcast_to(path_rows[None], (requests,) + path_rows.shape)], axis=1
    )
    blocks_kv = lax.all_to_all(outgoing, "bx", split_axis=0, concat_axis=0, tiled=True)
    tree_keys = group_rows[:, width_q : width_q + cache_width].reshape(
        1, 1, TREE_TOKENS, kv_local, HEAD_SIZE
    )
    tree_values = group_rows[:, width_q + cache_width :].reshape(
        1, 1, TREE_TOKENS, kv_local, HEAD_SIZE
    )
    reachable = ancestors(lax.dynamic_slice_in_dim(parents, my_request, 1, 0))
    own_reach = lax.dynamic_slice_in_dim(reachable, node_start, rows_dev, 1)
    draft_usable = (own_reach > 0.5)[None, :, None, None, :, :]
    draft_part = partial_softmax(local_queries, tree_keys, tree_values, draft_usable, score_scale)
    source_blocks = jnp.arange(blocks_kv.shape[0], dtype=jnp.int32) * ring + my_z
    limit = lengths[my_request] - source_blocks * block_len
    packed_out = block_attention(limit, group_rows, blocks_kv, width_q, block_len)
    head_count = width_q // HEAD_SIZE
    width_out = width_q
    moved = lax.all_to_all(
        packed_out.reshape(ring, rows_dev, -1), "bz", split_axis=0, concat_axis=0, tiled=True
    )
    parts = [
        moved[..., width_out + j * 2 * head_count : width_out + (j + 1) * 2 * head_count].astype(
            jnp.float32
        )
        for j in range(3)
    ]
    moved_stats = (parts[0] + parts[1]) + parts[2]
    cache_part = (
        moved[..., :width_out],
        moved_stats[..., :head_count],
        moved_stats[..., head_count:],
    )
    attention = merge_parts(cache_part, draft_part, HEAD_SIZE)
    every_row = gather_rows(attention, blk)
    partial = jnp.dot(every_row, out_weight, preferred_element_type=jnp.float32)
    out_rows = partial.shape[0] // kv_count
    arrived = lax.all_to_all(
        partial.reshape(kv_count, out_rows, partial.shape[1]),
        "kv",
        split_axis=0,
        concat_axis=0,
        tiled=True,
    )
    projected = jnp.sum(arrived, axis=0).astype(jnp.bfloat16)
    positions_here = my_block * block_len + jnp.arange(block_len, dtype=jnp.int32)
    offset = positions_here[None, :] - lengths[:, None]
    written = (offset >= 0) & (offset < accepted_count[:, None])
    path_all = blocks_kv[:, block_len:, :]
    new_cache_keys = place_rows(path_all[..., :cache_width], offset, written, cached_key_vectors)
    new_cache_values = place_rows(
        path_all[..., cache_width:], offset, written, cached_value_vectors
    )
    return (projected, new_cache_keys, new_cache_values)


def solution(mesh):
    kv_size, blk_size = mesh.devices.shape
    requests = 4
    ring = blk_size // requests
    grid_mesh = Mesh(mesh.devices.reshape(kv_size, requests, ring), ("kv", "bx", "bz"))
    blk = ("bx", "bz")
    return jax.shard_map(
        on_device,
        mesh=grid_mesh,
        in_specs=(
            P(blk, "kv"),
            P(blk, "kv"),
            P(blk, "kv"),
            P(None, blk, "kv"),
            P(None, blk, "kv"),
            P("kv", blk),
            P(),
            P(),
            P(),
            P(),
        ),
        out_specs=(P("kv", blk), P(None, blk, "kv"), P(None, blk, "kv")),
        check_vma=False,
    )
```

```python
import functools
import math

import jax
import jax.numpy as jnp
from jax import lax
from jax.sharding import Mesh, PartitionSpec as P
from jax.experimental import pallas as pl
from jax.experimental.pallas import tpu as pltpu

HEAD_SIZE = 128
TREE_TOKENS = 64
ACC = 8


NEG_FLOOR = -1e30


def ancestors(parent_rows):
    node_ids = jnp.arange(TREE_TOKENS, dtype=jnp.int32)
    parent_link = (
        (parent_rows[:, :, None] == node_ids[None, None, :]) & (node_ids[None, :, None] >= 1)
    ).astype(jnp.float32)
    reachable = jnp.eye(TREE_TOKENS, dtype=jnp.float32)[None] + parent_link
    for doubling in range((TREE_TOKENS - 1).bit_length()):
        reachable = jnp.minimum(
            reachable
            + jnp.einsum("rij,rjk->rik", reachable, reachable, precision=lax.Precision.HIGHEST),
            1.0,
        )
    return reachable


def partial_softmax(query_vectors, key_rows, value_rows, usable, score_scale):
    scores = (
        jnp.einsum(
            "rtkgh,rbpkh->brkgtp", query_vectors, key_rows, preferred_element_type=jnp.float32
        )
        * score_scale
    )
    scores = jnp.where(usable, scores, NEG_FLOOR)
    peak_score = jnp.max(scores, axis=-1)
    weights = jnp.where(usable, jnp.exp(scores - peak_score[..., None]), 0.0)
    weight_sum = jnp.sum(weights, axis=-1)
    weighted = jnp.einsum(
        "brkgtp,rbpkh->brtkgh",
        weights.astype(jnp.bfloat16),
        value_rows,
        preferred_element_type=jnp.float32,
    )
    block_count, req_count, kv_count, query_group_width, row_count = peak_score.shape
    weighted = weighted.reshape(
        block_count, req_count * row_count, kv_count * query_group_width * value_rows.shape[-1]
    )
    peak_score = peak_score.transpose(0, 1, 4, 2, 3).reshape(
        block_count, req_count * row_count, kv_count * query_group_width
    )
    weight_sum = weight_sum.transpose(0, 1, 4, 2, 3).reshape(
        block_count, req_count * row_count, kv_count * query_group_width
    )
    return (weighted, peak_score, weight_sum)


def merge_parts(cache_part, draft_part, head_dim):
    cache_out, cache_peak, cache_sum = cache_part
    draft_out, draft_peak, draft_sum = draft_part
    cache_out = cache_out.astype(jnp.float32)
    overall = jnp.maximum(jnp.max(cache_peak, axis=0), draft_peak[0])
    cache_factor = jnp.exp(cache_peak - overall[None])
    draft_factor = jnp.exp(draft_peak[0] - overall)
    denominator = jnp.sum(cache_factor * cache_sum, axis=0) + draft_factor * draft_sum[0]
    block_count, row_count, head_count = cache_peak.shape
    numerator = jnp.sum(
        cache_factor[..., None] * cache_out.reshape(block_count, row_count, head_count, head_dim),
        axis=0,
    )
    numerator = numerator + draft_factor[..., None] * draft_out[0].reshape(
        row_count, head_count, head_dim
    )
    return (
        (numerator / denominator[..., None])
        .reshape(row_count, head_count * head_dim)
        .astype(jnp.bfloat16)
    )


def place_rows(sources, slot_index, written, cache_rows):
    slot_ids = jnp.arange(sources.shape[1], dtype=jnp.int32)
    selector = ((slot_index[:, :, None] == slot_ids[None, None, :]) & written[:, :, None]).astype(
        jnp.bfloat16
    )
    placed = jnp.einsum(
        "rps,rsc->rpc", selector, sources, preferred_element_type=jnp.float32
    ).astype(jnp.bfloat16)
    return jnp.where(written[:, :, None], placed, cache_rows)


def split_three(x):
    hi = x.astype(jnp.bfloat16)
    rest = x - hi.astype(jnp.float32)
    mid = rest.astype(jnp.bfloat16)
    lo = (rest - mid.astype(jnp.float32)).astype(jnp.bfloat16)
    return hi, mid, lo


def block_attention_kernel(block_len, limit_ref, q_ref, kv_ref, out_ref, stats_ref):
    blocks = kv_ref.shape[0]
    rows = out_ref.shape[0]
    heads = stats_ref.shape[1] // 2
    score_scale = 1.0 / math.sqrt(HEAD_SIZE)
    q = jnp.concatenate(
        [q_ref[:, h * HEAD_SIZE : (h + 1) * HEAD_SIZE] for h in range(heads)], axis=0
    )
    scores = []
    valids = []
    for b in range(blocks):
        s = (
            lax.dot_general(
                q,
                kv_ref[b, :block_len, :HEAD_SIZE],
                (((1,), (1,)), ((), ())),
                preferred_element_type=jnp.float32,
            )
            * score_scale
        )
        valid = lax.broadcasted_iota(jnp.int32, s.shape, 1) < limit_ref[b]
        scores.append(jnp.where(valid, s, NEG_FLOOR))
        valids.append(valid)
    peak = jnp.max(scores[0], axis=1, keepdims=True)
    for s in scores[1:]:
        peak = jnp.maximum(peak, jnp.max(s, axis=1, keepdims=True))
    total = jnp.zeros_like(peak)
    out = jnp.zeros((q.shape[0], HEAD_SIZE), jnp.float32)
    for b in range(blocks):
        weights = jnp.where(valids[b], jnp.exp(scores[b] - peak), 0.0)
        total = total + jnp.sum(weights, axis=1, keepdims=True)
        out = out + jnp.dot(
            weights.astype(jnp.bfloat16),
            kv_ref[b, :block_len, HEAD_SIZE:],
            preferred_element_type=jnp.float32,
        )
    out = out.astype(out_ref.dtype)
    for h in range(heads):
        here = slice(h * rows, (h + 1) * rows)
        out_ref[:, h * HEAD_SIZE : (h + 1) * HEAD_SIZE] = out[here]
        stats_ref[:, h : h + 1] = peak[here]
        stats_ref[:, heads + h : heads + h + 1] = total[here]
    width = heads * HEAD_SIZE
    stats = stats_ref[...]
    for j, part in enumerate(split_three(stats)):
        out_ref[:, width + j * 2 * heads : width + (j + 1) * 2 * heads] = part


def block_attention(limit, group_rows, blocks_kv, width, block_len):
    rows = group_rows.shape[0]
    heads = width // HEAD_SIZE
    blocks = blocks_kv.shape[0]
    vmem = pl.BlockSpec(memory_space=pltpu.VMEM)
    return pl.pallas_call(
        functools.partial(block_attention_kernel, block_len),
        out_shape=jax.ShapeDtypeStruct((rows, width + 6 * heads), jnp.bfloat16),
        in_specs=[pl.BlockSpec(memory_space=pltpu.SMEM), vmem, vmem],
        out_specs=vmem,
        scratch_shapes=[pltpu.VMEM((rows, 2 * heads), jnp.float32)],
        cost_estimate=pl.CostEstimate(
            flops=4 * rows * heads * blocks * block_len * HEAD_SIZE,
            transcendentals=rows * heads * blocks * block_len,
            bytes_accessed=2 * (rows * width + 2 * blocks * block_len * HEAD_SIZE + rows * (width + 6 * heads)),
        ),
    )(limit, group_rows, blocks_kv)


def shifted(block, axis_name, shift):
    count = lax.axis_size(axis_name)
    return lax.ppermute(block, axis_name, [(i, (i + shift) % count) for i in range(count)])


def gather_rows(block, axis_name):
    count = lax.axis_size(axis_name)
    spread = jnp.broadcast_to(block[None], (count,) + block.shape)
    moved = lax.all_to_all(spread, axis_name, split_axis=0, concat_axis=0, tiled=True)
    return moved.reshape((count * block.shape[0],) + block.shape[1:])


def on_device(
    queries,
    draft_token_keys,
    draft_token_values,
    cached_key_vectors,
    cached_value_vectors,
    out_weight,
    lengths,
    parents,
    accepted_nodes,
    accepted_count,
):
    blk = ("bx", "bz")
    kv_count = lax.axis_size("kv")
    ring = lax.axis_size("bz")
    my_block = lax.axis_index(blk)
    my_x = lax.axis_index("bx")
    my_z = lax.axis_index("bz")
    rows_dev, width_q = queries.shape
    requests = lengths.shape[0]
    cache_width = cached_key_vectors.shape[2]
    kv_local = cache_width // HEAD_SIZE
    query_group_width = width_q // (kv_local * HEAD_SIZE)
    block_len = cached_key_vectors.shape[1]
    score_scale = 1.0 / math.sqrt(HEAD_SIZE)
    my_request = my_x
    node_start = my_z * rows_dev
    local_queries = queries.reshape(1, rows_dev, kv_local, query_group_width, HEAD_SIZE)
    own_draft = jnp.concatenate([draft_token_keys, draft_token_values], axis=1)
    group_rows = gather_rows(jnp.concatenate([queries, own_draft], axis=1), "bz")
    cache_pair = jnp.concatenate([cached_key_vectors, cached_value_vectors], axis=2)
    path_pick = (
        accepted_nodes[my_request][:, None] == jnp.arange(TREE_TOKENS, dtype=jnp.int32)[None, :]
    ).astype(jnp.bfloat16)
    path_rows = jnp.dot(
        path_pick, group_rows[:, width_q:], preferred_element_type=jnp.float32
    ).astype(jnp.bfloat16)
    lanes = cache_pair.shape[0]
    ahead = jnp.roll(cache_pair, -my_x, axis=0)
    blocks_kv = jnp.stack(
        [ahead[0]] + [shifted(ahead[k], "bx", k) for k in range(1, lanes)], axis=0
    )
    path_rel = jnp.stack(
        [path_rows] + [shifted(path_rows, "bx", k) for k in range(1, lanes)], axis=0
    )
    source_x = (my_x - jnp.arange(lanes, dtype=jnp.int32)) % lanes
    tree_keys = group_rows[:, width_q : width_q + cache_width].reshape(
        1, 1, TREE_TOKENS, kv_local, HEAD_SIZE
    )
    tree_values = group_rows[:, width_q + cache_width :].reshape(
        1, 1, TREE_TOKENS, kv_local, HEAD_SIZE
    )
    reachable = ancestors(lax.dynamic_slice_in_dim(parents, my_request, 1, 0))
    own_reach = lax.dynamic_slice_in_dim(reachable, node_start, rows_dev, 1)
    draft_usable = (own_reach > 0.5)[None, :, None, None, :, :]
    draft_part = partial_softmax(local_queries, tree_keys, tree_values, draft_usable, score_scale)
    source_blocks = source_x * ring + my_z
    limit = lengths[my_request] - source_blocks * block_len
    packed_out = block_attention(limit, group_rows, blocks_kv, width_q, block_len)
    head_count = width_q // HEAD_SIZE
    width_out = width_q
    moved = lax.all_to_all(
        packed_out.reshape(ring, rows_dev, -1), "bz", split_axis=0, concat_axis=0, tiled=True
    )
    parts = [
        moved[..., width_out + j * 2 * head_count : width_out + (j + 1) * 2 * head_count].astype(
            jnp.float32
        )
        for j in range(3)
    ]
    moved_stats = (parts[0] + parts[1]) + parts[2]
    cache_part = (
        moved[..., :width_out],
        moved_stats[..., :head_count],
        moved_stats[..., head_count:],
    )
    attention = merge_parts(cache_part, draft_part, HEAD_SIZE)
    every_row = gather_rows(attention, blk)
    partial = jnp.dot(every_row, out_weight, preferred_element_type=jnp.float32)
    out_rows = partial.shape[0] // kv_count
    arrived = lax.all_to_all(
        partial.reshape(kv_count, out_rows, partial.shape[1]),
        "kv",
        split_axis=0,
        concat_axis=0,
        tiled=True,
    )
    projected = jnp.sum(arrived, axis=0).astype(jnp.bfloat16)
    positions_here = my_block * block_len + jnp.arange(block_len, dtype=jnp.int32)
    offset = positions_here[None, :] - lengths[:, None]
    written = (offset >= 0) & (offset < accepted_count[:, None])
    path_all = jnp.roll(path_rel[(-jnp.arange(lanes)) % lanes], my_x, axis=0)
    new_cache_keys = place_rows(path_all[..., :cache_width], offset, written, cached_key_vectors)
    new_cache_values = place_rows(
        path_all[..., cache_width:], offset, written, cached_value_vectors
    )
    return (projected, new_cache_keys, new_cache_values)


def solution(mesh):
    kv_size, blk_size = mesh.devices.shape
    requests = 4
    ring = blk_size // requests
    grid_mesh = Mesh(mesh.devices.reshape(kv_size, requests, ring), ("kv", "bx", "bz"))
    blk = ("bx", "bz")
    return jax.shard_map(
        on_device,
        mesh=grid_mesh,
        in_specs=(
            P(blk, "kv"),
            P(blk, "kv"),
            P(blk, "kv"),
            P(None, blk, "kv"),
            P(None, blk, "kv"),
            P("kv", blk),
            P(),
            P(),
            P(),
            P(),
        ),
        out_specs=(P("kv", blk), P(None, blk, "kv"), P(None, blk, "kv")),
        check_vma=False,
    )
```

```python
import functools
import math

import jax
import jax.numpy as jnp
from jax import lax
from jax.sharding import Mesh, PartitionSpec as P
from jax.experimental import pallas as pl
from jax.experimental.pallas import tpu as pltpu

HEAD_SIZE = 128
TREE_TOKENS = 64
ACC = 8


NEG_FLOOR = -1e30


def ancestors(parent_rows):
    node_ids = jnp.arange(TREE_TOKENS, dtype=jnp.int32)
    parent_link = (
        (parent_rows[:, :, None] == node_ids[None, None, :]) & (node_ids[None, :, None] >= 1)
    ).astype(jnp.float32)
    reachable = jnp.eye(TREE_TOKENS, dtype=jnp.float32)[None] + parent_link
    for doubling in range((TREE_TOKENS - 1).bit_length()):
        reachable = jnp.minimum(
            reachable
            + jnp.einsum("rij,rjk->rik", reachable, reachable, precision=lax.Precision.HIGHEST),
            1.0,
        )
    return reachable


def partial_softmax(query_vectors, key_rows, value_rows, usable, score_scale):
    scores = (
        jnp.einsum(
            "rtkgh,rbpkh->brkgtp", query_vectors, key_rows, preferred_element_type=jnp.float32
        )
        * score_scale
    )
    scores = jnp.where(usable, scores, NEG_FLOOR)
    peak_score = jnp.max(scores, axis=-1)
    weights = jnp.where(usable, jnp.exp(scores - peak_score[..., None]), 0.0)
    weight_sum = jnp.sum(weights, axis=-1)
    weighted = jnp.einsum(
        "brkgtp,rbpkh->brtkgh",
        weights.astype(jnp.bfloat16),
        value_rows,
        preferred_element_type=jnp.float32,
    )
    block_count, req_count, kv_count, query_group_width, row_count = peak_score.shape
    weighted = weighted.reshape(
        block_count, req_count * row_count, kv_count * query_group_width * value_rows.shape[-1]
    )
    peak_score = peak_score.transpose(0, 1, 4, 2, 3).reshape(
        block_count, req_count * row_count, kv_count * query_group_width
    )
    weight_sum = weight_sum.transpose(0, 1, 4, 2, 3).reshape(
        block_count, req_count * row_count, kv_count * query_group_width
    )
    return (weighted, peak_score, weight_sum)


def merge_parts(cache_part, draft_part, head_dim):
    cache_out, cache_peak, cache_sum = cache_part
    draft_out, draft_peak, draft_sum = draft_part
    cache_out = cache_out.astype(jnp.float32)
    overall = jnp.maximum(jnp.max(cache_peak, axis=0), draft_peak[0])
    cache_factor = jnp.exp(cache_peak - overall[None])
    draft_factor = jnp.exp(draft_peak[0] - overall)
    denominator = jnp.sum(cache_factor * cache_sum, axis=0) + draft_factor * draft_sum[0]
    block_count, row_count, head_count = cache_peak.shape
    numerator = jnp.sum(
        cache_factor[..., None] * cache_out.reshape(block_count, row_count, head_count, head_dim),
        axis=0,
    )
    numerator = numerator + draft_factor[..., None] * draft_out[0].reshape(
        row_count, head_count, head_dim
    )
    return (
        (numerator / denominator[..., None])
        .reshape(row_count, head_count * head_dim)
        .astype(jnp.bfloat16)
    )


def place_rows(sources, slot_index, written, cache_rows):
    slot_ids = jnp.arange(sources.shape[1], dtype=jnp.int32)
    selector = ((slot_index[:, :, None] == slot_ids[None, None, :]) & written[:, :, None]).astype(
        jnp.bfloat16
    )
    placed = jnp.einsum(
        "rps,rsc->rpc", selector, sources, preferred_element_type=jnp.float32
    ).astype(jnp.bfloat16)
    return jnp.where(written[:, :, None], placed, cache_rows)


def split_three(x):
    hi = x.astype(jnp.bfloat16)
    rest = x - hi.astype(jnp.float32)
    mid = rest.astype(jnp.bfloat16)
    lo = (rest - mid.astype(jnp.float32)).astype(jnp.bfloat16)
    return hi, mid, lo


def block_attention_kernel(block_len, limit_ref, q_ref, *refs):
    kv_refs, (out_ref, stats_ref) = refs[:-2], refs[-2:]
    blocks = len(kv_refs)
    rows = out_ref.shape[0]
    heads = stats_ref.shape[1] // 2
    score_scale = 1.0 / math.sqrt(HEAD_SIZE)
    q = jnp.concatenate(
        [q_ref[:, h * HEAD_SIZE : (h + 1) * HEAD_SIZE] for h in range(heads)], axis=0
    )
    scores = []
    valids = []
    for b in range(blocks):
        s = (
            lax.dot_general(
                q,
                kv_refs[b][:block_len, :HEAD_SIZE],
                (((1,), (1,)), ((), ())),
                preferred_element_type=jnp.float32,
            )
            * score_scale
        )
        valid = lax.broadcasted_iota(jnp.int32, s.shape, 1) < limit_ref[b]
        scores.append(jnp.where(valid, s, NEG_FLOOR))
        valids.append(valid)
    peak = jnp.max(scores[0], axis=1, keepdims=True)
    for s in scores[1:]:
        peak = jnp.maximum(peak, jnp.max(s, axis=1, keepdims=True))
    total = jnp.zeros_like(peak)
    out = jnp.zeros((q.shape[0], HEAD_SIZE), jnp.float32)
    for b in range(blocks):
        weights = jnp.where(valids[b], jnp.exp(scores[b] - peak), 0.0)
        total = total + jnp.sum(weights, axis=1, keepdims=True)
        out = out + jnp.dot(
            weights.astype(jnp.bfloat16),
            kv_refs[b][:block_len, HEAD_SIZE:],
            preferred_element_type=jnp.float32,
        )
    out = out.astype(out_ref.dtype)
    for h in range(heads):
        here = slice(h * rows, (h + 1) * rows)
        out_ref[:, h * HEAD_SIZE : (h + 1) * HEAD_SIZE] = out[here]
        stats_ref[:, h : h + 1] = peak[here]
        stats_ref[:, heads + h : heads + h + 1] = total[here]
    width = heads * HEAD_SIZE
    stats = stats_ref[...]
    for j, part in enumerate(split_three(stats)):
        out_ref[:, width + j * 2 * heads : width + (j + 1) * 2 * heads] = part


def block_attention(limit, group_rows, blocks_kv, width, block_len):
    rows = group_rows.shape[0]
    heads = width // HEAD_SIZE
    blocks = len(blocks_kv)
    vmem = pl.BlockSpec(memory_space=pltpu.VMEM)
    return pl.pallas_call(
        functools.partial(block_attention_kernel, block_len),
        out_shape=jax.ShapeDtypeStruct((rows, width + 6 * heads), jnp.bfloat16),
        in_specs=[pl.BlockSpec(memory_space=pltpu.SMEM), vmem] + [vmem] * blocks,
        out_specs=vmem,
        scratch_shapes=[pltpu.VMEM((rows, 2 * heads), jnp.float32)],
        cost_estimate=pl.CostEstimate(
            flops=4 * rows * heads * blocks * block_len * HEAD_SIZE,
            transcendentals=rows * heads * blocks * block_len,
            bytes_accessed=2 * (rows * width + 2 * blocks * block_len * HEAD_SIZE + rows * (width + 6 * heads)),
        ),
    )(limit, group_rows, *blocks_kv)


def shifted(block, axis_name, shift):
    count = lax.axis_size(axis_name)
    return lax.ppermute(block, axis_name, [(i, (i + shift) % count) for i in range(count)])


def gather_rows(block, axis_name):
    count = lax.axis_size(axis_name)
    spread = jnp.broadcast_to(block[None], (count,) + block.shape)
    moved = lax.all_to_all(spread, axis_name, split_axis=0, concat_axis=0, tiled=True)
    return moved.reshape((count * block.shape[0],) + block.shape[1:])


def on_device(
    queries,
    draft_token_keys,
    draft_token_values,
    cached_key_vectors,
    cached_value_vectors,
    out_weight,
    lengths,
    parents,
    accepted_nodes,
    accepted_count,
):
    blk = ("bx", "bz")
    kv_count = lax.axis_size("kv")
    ring = lax.axis_size("bz")
    my_block = lax.axis_index(blk)
    my_x = lax.axis_index("bx")
    my_z = lax.axis_index("bz")
    rows_dev, width_q = queries.shape
    requests = lengths.shape[0]
    cache_width = cached_key_vectors.shape[2]
    kv_local = cache_width // HEAD_SIZE
    query_group_width = width_q // (kv_local * HEAD_SIZE)
    block_len = cached_key_vectors.shape[1]
    score_scale = 1.0 / math.sqrt(HEAD_SIZE)
    my_request = my_x
    node_start = my_z * rows_dev
    local_queries = queries.reshape(1, rows_dev, kv_local, query_group_width, HEAD_SIZE)
    own_draft = jnp.concatenate([draft_token_keys, draft_token_values], axis=1)
    group_rows = gather_rows(jnp.concatenate([queries, own_draft], axis=1), "bz")
    cache_pair = jnp.concatenate([cached_key_vectors, cached_value_vectors], axis=2)
    path_pick = (
        accepted_nodes[my_request][:, None] == jnp.arange(TREE_TOKENS, dtype=jnp.int32)[None, :]
    ).astype(jnp.bfloat16)
    path_rows = jnp.dot(
        path_pick, group_rows[:, width_q:], preferred_element_type=jnp.float32
    ).astype(jnp.bfloat16)
    lanes = cache_pair.shape[0]
    ahead = jnp.roll(cache_pair, -my_x, axis=0)
    blocks_kv = [ahead[0]] + [shifted(ahead[k], "bx", k) for k in range(1, lanes)]
    path_rel = jnp.stack(
        [path_rows] + [shifted(path_rows, "bx", k) for k in range(1, lanes)], axis=0
    )
    source_x = (my_x - jnp.arange(lanes, dtype=jnp.int32)) % lanes
    tree_keys = group_rows[:, width_q : width_q + cache_width].reshape(
        1, 1, TREE_TOKENS, kv_local, HEAD_SIZE
    )
    tree_values = group_rows[:, width_q + cache_width :].reshape(
        1, 1, TREE_TOKENS, kv_local, HEAD_SIZE
    )
    reachable = ancestors(lax.dynamic_slice_in_dim(parents, my_request, 1, 0))
    own_reach = lax.dynamic_slice_in_dim(reachable, node_start, rows_dev, 1)
    draft_usable = (own_reach > 0.5)[None, :, None, None, :, :]
    draft_part = partial_softmax(local_queries, tree_keys, tree_values, draft_usable, score_scale)
    source_blocks = source_x * ring + my_z
    limit = lengths[my_request] - source_blocks * block_len
    packed_out = block_attention(limit, group_rows, blocks_kv, width_q, block_len)
    head_count = width_q // HEAD_SIZE
    width_out = width_q
    moved = lax.all_to_all(
        packed_out.reshape(ring, rows_dev, -1), "bz", split_axis=0, concat_axis=0, tiled=True
    )
    parts = [
        moved[..., width_out + j * 2 * head_count : width_out + (j + 1) * 2 * head_count].astype(
            jnp.float32
        )
        for j in range(3)
    ]
    moved_stats = (parts[0] + parts[1]) + parts[2]
    cache_part = (
        moved[..., :width_out],
        moved_stats[..., :head_count],
        moved_stats[..., head_count:],
    )
    attention = merge_parts(cache_part, draft_part, HEAD_SIZE)
    every_row = gather_rows(attention, blk)
    partial = jnp.dot(every_row, out_weight, preferred_element_type=jnp.float32)
    out_rows = partial.shape[0] // kv_count
    arrived = lax.all_to_all(
        partial.reshape(kv_count, out_rows, partial.shape[1]),
        "kv",
        split_axis=0,
        concat_axis=0,
        tiled=True,
    )
    projected = jnp.sum(arrived, axis=0).astype(jnp.bfloat16)
    positions_here = my_block * block_len + jnp.arange(block_len, dtype=jnp.int32)
    offset = positions_here[None, :] - lengths[:, None]
    written = (offset >= 0) & (offset < accepted_count[:, None])
    path_all = jnp.roll(path_rel[(-jnp.arange(lanes)) % lanes], my_x, axis=0)
    new_cache_keys = place_rows(path_all[..., :cache_width], offset, written, cached_key_vectors)
    new_cache_values = place_rows(
        path_all[..., cache_width:], offset, written, cached_value_vectors
    )
    return (projected, new_cache_keys, new_cache_values)


def solution(mesh):
    kv_size, blk_size = mesh.devices.shape
    requests = 4
    ring = blk_size // requests
    grid_mesh = Mesh(mesh.devices.reshape(kv_size, requests, ring), ("kv", "bx", "bz"))
    blk = ("bx", "bz")
    return jax.shard_map(
        on_device,
        mesh=grid_mesh,
        in_specs=(
            P(blk, "kv"),
            P(blk, "kv"),
            P(blk, "kv"),
            P(None, blk, "kv"),
            P(None, blk, "kv"),
            P("kv", blk),
            P(),
            P(),
            P(),
            P(),
        ),
        out_specs=(P("kv", blk), P(None, blk, "kv"), P(None, blk, "kv")),
        check_vma=False,
    )
```

```python
import functools
import math

import jax
import jax.numpy as jnp
from jax import lax
from jax.sharding import Mesh, PartitionSpec as P
from jax.experimental import pallas as pl
from jax.experimental.pallas import tpu as pltpu

HEAD_SIZE = 128
TREE_TOKENS = 64
ACC = 8


NEG_FLOOR = -1e30


def ancestors(parent_rows):
    node_ids = jnp.arange(TREE_TOKENS, dtype=jnp.int32)
    parent_link = (
        (parent_rows[:, :, None] == node_ids[None, None, :]) & (node_ids[None, :, None] >= 1)
    ).astype(jnp.float32)
    reachable = jnp.eye(TREE_TOKENS, dtype=jnp.float32)[None] + parent_link
    for doubling in range((TREE_TOKENS - 1).bit_length()):
        reachable = jnp.minimum(
            reachable
            + jnp.einsum("rij,rjk->rik", reachable, reachable, precision=lax.Precision.HIGHEST),
            1.0,
        )
    return reachable


def partial_softmax(query_vectors, key_rows, value_rows, usable, score_scale):
    scores = (
        jnp.einsum(
            "rtkgh,rbpkh->brkgtp", query_vectors, key_rows, preferred_element_type=jnp.float32
        )
        * score_scale
    )
    scores = jnp.where(usable, scores, NEG_FLOOR)
    peak_score = jnp.max(scores, axis=-1)
    weights = jnp.where(usable, jnp.exp(scores - peak_score[..., None]), 0.0)
    weight_sum = jnp.sum(weights, axis=-1)
    weighted = jnp.einsum(
        "brkgtp,rbpkh->brtkgh",
        weights.astype(jnp.bfloat16),
        value_rows,
        preferred_element_type=jnp.float32,
    )
    block_count, req_count, kv_count, query_group_width, row_count = peak_score.shape
    weighted = weighted.reshape(
        block_count, req_count * row_count, kv_count * query_group_width * value_rows.shape[-1]
    )
    peak_score = peak_score.transpose(0, 1, 4, 2, 3).reshape(
        block_count, req_count * row_count, kv_count * query_group_width
    )
    weight_sum = weight_sum.transpose(0, 1, 4, 2, 3).reshape(
        block_count, req_count * row_count, kv_count * query_group_width
    )
    return (weighted, peak_score, weight_sum)


def merge_parts(cache_part, draft_part, head_dim):
    cache_out, cache_peak, cache_sum = cache_part
    draft_out, draft_peak, draft_sum = draft_part
    cache_out = cache_out.astype(jnp.float32)
    overall = jnp.maximum(jnp.max(cache_peak, axis=0), draft_peak[0])
    cache_factor = jnp.exp(cache_peak - overall[None])
    draft_factor = jnp.exp(draft_peak[0] - overall)
    denominator = jnp.sum(cache_factor * cache_sum, axis=0) + draft_factor * draft_sum[0]
    block_count, row_count, head_count = cache_peak.shape
    numerator = jnp.sum(
        cache_factor[..., None] * cache_out.reshape(block_count, row_count, head_count, head_dim),
        axis=0,
    )
    numerator = numerator + draft_factor[..., None] * draft_out[0].reshape(
        row_count, head_count, head_dim
    )
    return (
        (numerator / denominator[..., None])
        .reshape(row_count, head_count * head_dim)
        .astype(jnp.bfloat16)
    )


def place_rows(sources, slot_index, written, cache_rows):
    slot_ids = jnp.arange(sources.shape[1], dtype=jnp.int32)
    selector = ((slot_index[:, :, None] == slot_ids[None, None, :]) & written[:, :, None]).astype(
        jnp.bfloat16
    )
    placed = jnp.einsum(
        "rps,rsc->rpc", selector, sources, preferred_element_type=jnp.float32
    ).astype(jnp.bfloat16)
    return jnp.where(written[:, :, None], placed, cache_rows)


def split_three(x):
    hi = x.astype(jnp.bfloat16)
    rest = x - hi.astype(jnp.float32)
    mid = rest.astype(jnp.bfloat16)
    lo = (rest - mid.astype(jnp.float32)).astype(jnp.bfloat16)
    return hi, mid, lo


def block_attention_kernel(block_len, limit_ref, q_ref, *refs):
    kv_refs, (out_ref, stats_ref) = refs[:-2], refs[-2:]
    blocks = len(kv_refs)
    rows = out_ref.shape[0]
    heads = stats_ref.shape[1] // 2
    score_scale = 1.0 / math.sqrt(HEAD_SIZE)
    q = jnp.concatenate(
        [q_ref[:, h * HEAD_SIZE : (h + 1) * HEAD_SIZE] for h in range(heads)], axis=0
    )
    scores = []
    valids = []
    for b in range(blocks):
        s = (
            lax.dot_general(
                q,
                kv_refs[b][:block_len, :HEAD_SIZE],
                (((1,), (1,)), ((), ())),
                preferred_element_type=jnp.float32,
            )
            * score_scale
        )
        valid = lax.broadcasted_iota(jnp.int32, s.shape, 1) < limit_ref[b]
        scores.append(jnp.where(valid, s, NEG_FLOOR))
        valids.append(valid)
    peak = jnp.max(scores[0], axis=1, keepdims=True)
    for s in scores[1:]:
        peak = jnp.maximum(peak, jnp.max(s, axis=1, keepdims=True))
    total = jnp.zeros_like(peak)
    out = jnp.zeros((q.shape[0], HEAD_SIZE), jnp.float32)
    for b in range(blocks):
        weights = jnp.where(valids[b], jnp.exp(scores[b] - peak), 0.0)
        total = total + jnp.sum(weights, axis=1, keepdims=True)
        out = out + jnp.dot(
            weights.astype(jnp.bfloat16),
            kv_refs[b][:block_len, HEAD_SIZE:],
            preferred_element_type=jnp.float32,
        )
    out = out.astype(out_ref.dtype)
    for h in range(heads):
        here = slice(h * rows, (h + 1) * rows)
        out_ref[:, h * HEAD_SIZE : (h + 1) * HEAD_SIZE] = out[here]
        stats_ref[:, h : h + 1] = peak[here]
        stats_ref[:, heads + h : heads + h + 1] = total[here]
    width = heads * HEAD_SIZE
    stats = stats_ref[...]
    for j, part in enumerate(split_three(stats)):
        out_ref[:, width + j * 2 * heads : width + (j + 1) * 2 * heads] = part


def block_attention(limit, group_rows, blocks_kv, width, block_len):
    rows = group_rows.shape[0]
    heads = width // HEAD_SIZE
    blocks = len(blocks_kv)
    vmem = pl.BlockSpec(memory_space=pltpu.VMEM)
    return pl.pallas_call(
        functools.partial(block_attention_kernel, block_len),
        out_shape=jax.ShapeDtypeStruct((rows, width + 6 * heads), jnp.bfloat16),
        in_specs=[pl.BlockSpec(memory_space=pltpu.SMEM), vmem] + [vmem] * blocks,
        out_specs=vmem,
        scratch_shapes=[pltpu.VMEM((rows, 2 * heads), jnp.float32)],
        cost_estimate=pl.CostEstimate(
            flops=4 * rows * heads * blocks * block_len * HEAD_SIZE,
            transcendentals=rows * heads * blocks * block_len,
            bytes_accessed=2 * (rows * width + 2 * blocks * block_len * HEAD_SIZE + rows * (width + 6 * heads)),
        ),
    )(limit, group_rows, *blocks_kv)


def shifted(block, axis_name, shift):
    count = lax.axis_size(axis_name)
    return lax.ppermute(block, axis_name, [(i, (i + shift) % count) for i in range(count)])


def spread_kernel(*refs):
    pieces, out_ref = refs[:-1], refs[-1]
    count = out_ref.shape[0]
    start = 0
    for piece in pieces:
        width = piece.shape[1]
        out_ref[:, :, start : start + width] = jnp.broadcast_to(
            piece[...][None], (count,) + piece.shape
        )
        start += width


def gather_rows(pieces, axis_name):
    count = lax.axis_size(axis_name)
    rows = pieces[0].shape[0]
    width = sum(piece.shape[1] for piece in pieces)
    vmem = pl.BlockSpec(memory_space=pltpu.VMEM)
    spread = pl.pallas_call(
        spread_kernel,
        out_shape=jax.ShapeDtypeStruct((count, rows, width), pieces[0].dtype),
        in_specs=[vmem] * len(pieces),
        out_specs=vmem,
        cost_estimate=pl.CostEstimate(
            flops=0, transcendentals=0, bytes_accessed=2 * (count + 1) * rows * width
        ),
    )(*pieces)
    moved = lax.all_to_all(spread, axis_name, split_axis=0, concat_axis=0, tiled=True)
    return moved.reshape((count * rows, width))


def on_device(
    queries,
    draft_token_keys,
    draft_token_values,
    cached_key_vectors,
    cached_value_vectors,
    out_weight,
    lengths,
    parents,
    accepted_nodes,
    accepted_count,
):
    blk = ("bx", "bz")
    kv_count = lax.axis_size("kv")
    ring = lax.axis_size("bz")
    my_block = lax.axis_index(blk)
    my_x = lax.axis_index("bx")
    my_z = lax.axis_index("bz")
    rows_dev, width_q = queries.shape
    requests = lengths.shape[0]
    cache_width = cached_key_vectors.shape[2]
    kv_local = cache_width // HEAD_SIZE
    query_group_width = width_q // (kv_local * HEAD_SIZE)
    block_len = cached_key_vectors.shape[1]
    score_scale = 1.0 / math.sqrt(HEAD_SIZE)
    my_request = my_x
    node_start = my_z * rows_dev
    local_queries = queries.reshape(1, rows_dev, kv_local, query_group_width, HEAD_SIZE)
    group_rows = gather_rows([queries, draft_token_keys, draft_token_values], "bz")
    cache_pair = jnp.concatenate([cached_key_vectors, cached_value_vectors], axis=2)
    path_pick = (
        accepted_nodes[my_request][:, None] == jnp.arange(TREE_TOKENS, dtype=jnp.int32)[None, :]
    ).astype(jnp.bfloat16)
    path_rows = jnp.dot(
        path_pick, group_rows[:, width_q:], preferred_element_type=jnp.float32
    ).astype(jnp.bfloat16)
    lanes = cache_pair.shape[0]
    ahead = jnp.roll(cache_pair, -my_x, axis=0)
    blocks_kv = [ahead[0]] + [shifted(ahead[k], "bx", k) for k in range(1, lanes)]
    path_rel = jnp.stack(
        [path_rows] + [shifted(path_rows, "bx", k) for k in range(1, lanes)], axis=0
    )
    source_x = (my_x - jnp.arange(lanes, dtype=jnp.int32)) % lanes
    tree_keys = group_rows[:, width_q : width_q + cache_width].reshape(
        1, 1, TREE_TOKENS, kv_local, HEAD_SIZE
    )
    tree_values = group_rows[:, width_q + cache_width :].reshape(
        1, 1, TREE_TOKENS, kv_local, HEAD_SIZE
    )
    reachable = ancestors(lax.dynamic_slice_in_dim(parents, my_request, 1, 0))
    own_reach = lax.dynamic_slice_in_dim(reachable, node_start, rows_dev, 1)
    draft_usable = (own_reach > 0.5)[None, :, None, None, :, :]
    draft_part = partial_softmax(local_queries, tree_keys, tree_values, draft_usable, score_scale)
    source_blocks = source_x * ring + my_z
    limit = lengths[my_request] - source_blocks * block_len
    packed_out = block_attention(limit, group_rows, blocks_kv, width_q, block_len)
    head_count = width_q // HEAD_SIZE
    width_out = width_q
    moved = lax.all_to_all(
        packed_out.reshape(ring, rows_dev, -1), "bz", split_axis=0, concat_axis=0, tiled=True
    )
    parts = [
        moved[..., width_out + j * 2 * head_count : width_out + (j + 1) * 2 * head_count].astype(
            jnp.float32
        )
        for j in range(3)
    ]
    moved_stats = (parts[0] + parts[1]) + parts[2]
    cache_part = (
        moved[..., :width_out],
        moved_stats[..., :head_count],
        moved_stats[..., head_count:],
    )
    attention = merge_parts(cache_part, draft_part, HEAD_SIZE)
    every_row = gather_rows([attention], blk)
    partial = jnp.dot(every_row, out_weight, preferred_element_type=jnp.float32)
    out_rows = partial.shape[0] // kv_count
    arrived = lax.all_to_all(
        partial.reshape(kv_count, out_rows, partial.shape[1]),
        "kv",
        split_axis=0,
        concat_axis=0,
        tiled=True,
    )
    projected = jnp.sum(arrived, axis=0).astype(jnp.bfloat16)
    positions_here = my_block * block_len + jnp.arange(block_len, dtype=jnp.int32)
    offset = positions_here[None, :] - lengths[:, None]
    written = (offset >= 0) & (offset < accepted_count[:, None])
    path_all = jnp.roll(path_rel[(-jnp.arange(lanes)) % lanes], my_x, axis=0)
    new_cache_keys = place_rows(path_all[..., :cache_width], offset, written, cached_key_vectors)
    new_cache_values = place_rows(
        path_all[..., cache_width:], offset, written, cached_value_vectors
    )
    return (projected, new_cache_keys, new_cache_values)


def solution(mesh):
    kv_size, blk_size = mesh.devices.shape
    requests = 4
    ring = blk_size // requests
    grid_mesh = Mesh(mesh.devices.reshape(kv_size, requests, ring), ("kv", "bx", "bz"))
    blk = ("bx", "bz")
    return jax.shard_map(
        on_device,
        mesh=grid_mesh,
        in_specs=(
            P(blk, "kv"),
            P(blk, "kv"),
            P(blk, "kv"),
            P(None, blk, "kv"),
            P(None, blk, "kv"),
            P("kv", blk),
            P(),
            P(),
            P(),
            P(),
        ),
        out_specs=(P("kv", blk), P(None, blk, "kv"), P(None, blk, "kv")),
        check_vma=False,
    )
```

```python
import functools
import math

import jax
import jax.numpy as jnp
from jax import lax
from jax.sharding import Mesh, PartitionSpec as P
from jax.experimental import pallas as pl
from jax.experimental.pallas import tpu as pltpu

HEAD_SIZE = 128
TREE_TOKENS = 64
ACC = 8


NEG_FLOOR = -1e30


def ancestors(parent_rows):
    node_ids = jnp.arange(TREE_TOKENS, dtype=jnp.int32)
    parent_link = (
        (parent_rows[:, :, None] == node_ids[None, None, :]) & (node_ids[None, :, None] >= 1)
    ).astype(jnp.float32)
    reachable = jnp.eye(TREE_TOKENS, dtype=jnp.float32)[None] + parent_link
    for doubling in range((TREE_TOKENS - 1).bit_length()):
        reachable = jnp.minimum(
            reachable
            + jnp.einsum("rij,rjk->rik", reachable, reachable, precision=lax.Precision.HIGHEST),
            1.0,
        )
    return reachable


def partial_softmax(query_vectors, key_rows, value_rows, usable, score_scale):
    scores = (
        jnp.einsum(
            "rtkgh,rbpkh->brkgtp", query_vectors, key_rows, preferred_element_type=jnp.float32
        )
        * score_scale
    )
    scores = jnp.where(usable, scores, NEG_FLOOR)
    peak_score = jnp.max(scores, axis=-1)
    weights = jnp.where(usable, jnp.exp(scores - peak_score[..., None]), 0.0)
    weight_sum = jnp.sum(weights, axis=-1)
    weighted = jnp.einsum(
        "brkgtp,rbpkh->brtkgh",
        weights.astype(jnp.bfloat16),
        value_rows,
        preferred_element_type=jnp.float32,
    )
    block_count, req_count, kv_count, query_group_width, row_count = peak_score.shape
    weighted = weighted.reshape(
        block_count, req_count * row_count, kv_count * query_group_width * value_rows.shape[-1]
    )
    peak_score = peak_score.transpose(0, 1, 4, 2, 3).reshape(
        block_count, req_count * row_count, kv_count * query_group_width
    )
    weight_sum = weight_sum.transpose(0, 1, 4, 2, 3).reshape(
        block_count, req_count * row_count, kv_count * query_group_width
    )
    return (weighted, peak_score, weight_sum)


def merge_parts(cache_part, draft_part, head_dim):
    cache_out, cache_peak, cache_sum = cache_part
    draft_out, draft_peak, draft_sum = draft_part
    cache_out = cache_out.astype(jnp.float32)
    overall = jnp.maximum(jnp.max(cache_peak, axis=0), draft_peak[0])
    cache_factor = jnp.exp(cache_peak - overall[None])
    draft_factor = jnp.exp(draft_peak[0] - overall)
    denominator = jnp.sum(cache_factor * cache_sum, axis=0) + draft_factor * draft_sum[0]
    block_count, row_count, head_count = cache_peak.shape
    numerator = jnp.sum(
        cache_factor[..., None] * cache_out.reshape(block_count, row_count, head_count, head_dim),
        axis=0,
    )
    numerator = numerator + draft_factor[..., None] * draft_out[0].reshape(
        row_count, head_count, head_dim
    )
    return (
        (numerator / denominator[..., None])
        .reshape(row_count, head_count * head_dim)
        .astype(jnp.bfloat16)
    )


def place_rows(sources, slot_index, written, cache_rows):
    slot_ids = jnp.arange(sources.shape[1], dtype=jnp.int32)
    selector = ((slot_index[:, :, None] == slot_ids[None, None, :]) & written[:, :, None]).astype(
        jnp.bfloat16
    )
    placed = jnp.einsum(
        "rps,rsc->rpc", selector, sources, preferred_element_type=jnp.float32
    ).astype(jnp.bfloat16)
    return jnp.where(written[:, :, None], placed, cache_rows)


def split_three(x):
    hi = x.astype(jnp.bfloat16)
    rest = x - hi.astype(jnp.float32)
    mid = rest.astype(jnp.bfloat16)
    lo = (rest - mid.astype(jnp.float32)).astype(jnp.bfloat16)
    return hi, mid, lo


def block_attention_kernel(block_len, limit_ref, q_ref, *refs):
    kv_refs, (out_ref, stats_ref) = refs[:-2], refs[-2:]
    blocks = len(kv_refs)
    rows = out_ref.shape[0]
    heads = stats_ref.shape[1] // 2
    score_scale = 1.0 / math.sqrt(HEAD_SIZE)
    q = jnp.concatenate(
        [q_ref[:, h * HEAD_SIZE : (h + 1) * HEAD_SIZE] for h in range(heads)], axis=0
    )
    scores = []
    valids = []
    for b in range(blocks):
        s = (
            lax.dot_general(
                q,
                kv_refs[b][:block_len, :HEAD_SIZE],
                (((1,), (1,)), ((), ())),
                preferred_element_type=jnp.float32,
            )
            * score_scale
        )
        valid = lax.broadcasted_iota(jnp.int32, s.shape, 1) < limit_ref[b]
        scores.append(jnp.where(valid, s, NEG_FLOOR))
        valids.append(valid)
    peak = jnp.max(scores[0], axis=1, keepdims=True)
    for s in scores[1:]:
        peak = jnp.maximum(peak, jnp.max(s, axis=1, keepdims=True))
    total = jnp.zeros_like(peak)
    out = jnp.zeros((q.shape[0], HEAD_SIZE), jnp.float32)
    for b in range(blocks):
        weights = jnp.where(valids[b], jnp.exp(scores[b] - peak), 0.0)
        total = total + jnp.sum(weights, axis=1, keepdims=True)
        out = out + jnp.dot(
            weights.astype(jnp.bfloat16),
            kv_refs[b][:block_len, HEAD_SIZE:],
            preferred_element_type=jnp.float32,
        )
    out = out.astype(out_ref.dtype)
    for h in range(heads):
        here = slice(h * rows, (h + 1) * rows)
        out_ref[:, h * HEAD_SIZE : (h + 1) * HEAD_SIZE] = out[here]
        stats_ref[:, h : h + 1] = peak[here]
        stats_ref[:, heads + h : heads + h + 1] = total[here]
    width = heads * HEAD_SIZE
    stats = stats_ref[...]
    for j, part in enumerate(split_three(stats)):
        out_ref[:, width + j * 2 * heads : width + (j + 1) * 2 * heads] = part


def block_attention(limit, group_rows, blocks_kv, width, block_len):
    rows = group_rows.shape[0]
    heads = width // HEAD_SIZE
    blocks = len(blocks_kv)
    vmem = pl.BlockSpec(memory_space=pltpu.VMEM)
    return pl.pallas_call(
        functools.partial(block_attention_kernel, block_len),
        out_shape=jax.ShapeDtypeStruct((rows, width + 6 * heads), jnp.bfloat16),
        in_specs=[pl.BlockSpec(memory_space=pltpu.SMEM), vmem] + [vmem] * blocks,
        out_specs=vmem,
        scratch_shapes=[pltpu.VMEM((rows, 2 * heads), jnp.float32)],
        cost_estimate=pl.CostEstimate(
            flops=4 * rows * heads * blocks * block_len * HEAD_SIZE,
            transcendentals=rows * heads * blocks * block_len,
            bytes_accessed=2 * (rows * width + 2 * blocks * block_len * HEAD_SIZE + rows * (width + 6 * heads)),
        ),
    )(limit, group_rows, *blocks_kv)


def shifted(block, axis_name, shift):
    count = lax.axis_size(axis_name)
    return lax.ppermute(block, axis_name, [(i, (i + shift) % count) for i in range(count)])


def merge_kernel(moved_ref, dout_ref, dpeak_ref, dsum_ref, out_ref):
    sources = moved_ref.shape[0]
    width = dout_ref.shape[1]
    heads = width // HEAD_SIZE
    peaks, sums = [], []
    for s in range(sources):
        part = [
            moved_ref[s, :, width + j * 2 * heads : width + (j + 1) * 2 * heads].astype(jnp.float32)
            for j in range(3)
        ]
        stats = (part[0] + part[1]) + part[2]
        peaks.append(stats[:, :heads])
        sums.append(stats[:, heads:])
    draft_peak = dpeak_ref[...]
    overall = peaks[0]
    for peak in peaks[1:]:
        overall = jnp.maximum(overall, peak)
    overall = jnp.maximum(overall, draft_peak)
    factors = [jnp.exp(peak - overall) for peak in peaks]
    draft_factor = jnp.exp(draft_peak - overall)
    den = factors[0] * sums[0]
    for factor, total in zip(factors[1:], sums[1:]):
        den = den + factor * total
    den = den + draft_factor * dsum_ref[...]
    count = out_ref.shape[0]
    for h in range(heads):
        cols = slice(h * HEAD_SIZE, (h + 1) * HEAD_SIZE)
        num = factors[0][:, h : h + 1] * moved_ref[0, :, cols].astype(jnp.float32)
        for s in range(1, sources):
            num = num + factors[s][:, h : h + 1] * moved_ref[s, :, cols].astype(jnp.float32)
        num = num + draft_factor[:, h : h + 1] * dout_ref[:, cols]
        att = (num / den[:, h : h + 1]).astype(out_ref.dtype)
        out_ref[:, :, cols] = jnp.broadcast_to(att[None], (count,) + att.shape)


def merge_and_spread(moved, draft_part, count):
    draft_out, draft_peak, draft_sum = draft_part
    rows = moved.shape[1]
    width = draft_out.shape[-1]
    vmem = pl.BlockSpec(memory_space=pltpu.VMEM)
    return pl.pallas_call(
        merge_kernel,
        out_shape=jax.ShapeDtypeStruct((count, rows, width), jnp.bfloat16),
        in_specs=[vmem] * 4,
        out_specs=vmem,
        cost_estimate=pl.CostEstimate(
            flops=4 * moved.shape[0] * rows * width,
            transcendentals=2 * moved.shape[0] * rows * width // HEAD_SIZE,
            bytes_accessed=2 * moved.size + 4 * rows * width + 2 * count * rows * width,
        ),
    )(moved, draft_out[0], draft_peak[0], draft_sum[0])


def gather_rows(block, axis_name):
    count = lax.axis_size(axis_name)
    spread = jnp.broadcast_to(block[None], (count,) + block.shape)
    moved = lax.all_to_all(spread, axis_name, split_axis=0, concat_axis=0, tiled=True)
    return moved.reshape((count * block.shape[0],) + block.shape[1:])


def on_device(
    queries,
    draft_token_keys,
    draft_token_values,
    cached_key_vectors,
    cached_value_vectors,
    out_weight,
    lengths,
    parents,
    accepted_nodes,
    accepted_count,
):
    blk = ("bx", "bz")
    kv_count = lax.axis_size("kv")
    ring = lax.axis_size("bz")
    my_block = lax.axis_index(blk)
    my_x = lax.axis_index("bx")
    my_z = lax.axis_index("bz")
    rows_dev, width_q = queries.shape
    requests = lengths.shape[0]
    cache_width = cached_key_vectors.shape[2]
    kv_local = cache_width // HEAD_SIZE
    query_group_width = width_q // (kv_local * HEAD_SIZE)
    block_len = cached_key_vectors.shape[1]
    score_scale = 1.0 / math.sqrt(HEAD_SIZE)
    my_request = my_x
    node_start = my_z * rows_dev
    local_queries = queries.reshape(1, rows_dev, kv_local, query_group_width, HEAD_SIZE)
    own_draft = jnp.concatenate([draft_token_keys, draft_token_values], axis=1)
    group_rows = gather_rows(jnp.concatenate([queries, own_draft], axis=1), "bz")
    cache_pair = jnp.concatenate([cached_key_vectors, cached_value_vectors], axis=2)
    path_pick = (
        accepted_nodes[my_request][:, None] == jnp.arange(TREE_TOKENS, dtype=jnp.int32)[None, :]
    ).astype(jnp.bfloat16)
    path_rows = jnp.dot(
        path_pick, group_rows[:, width_q:], preferred_element_type=jnp.float32
    ).astype(jnp.bfloat16)
    lanes = cache_pair.shape[0]
    ahead = jnp.roll(cache_pair, -my_x, axis=0)
    blocks_kv = [ahead[0]] + [shifted(ahead[k], "bx", k) for k in range(1, lanes)]
    path_rel = jnp.stack(
        [path_rows] + [shifted(path_rows, "bx", k) for k in range(1, lanes)], axis=0
    )
    source_x = (my_x - jnp.arange(lanes, dtype=jnp.int32)) % lanes
    tree_keys = group_rows[:, width_q : width_q + cache_width].reshape(
        1, 1, TREE_TOKENS, kv_local, HEAD_SIZE
    )
    tree_values = group_rows[:, width_q + cache_width :].reshape(
        1, 1, TREE_TOKENS, kv_local, HEAD_SIZE
    )
    reachable = ancestors(lax.dynamic_slice_in_dim(parents, my_request, 1, 0))
    own_reach = lax.dynamic_slice_in_dim(reachable, node_start, rows_dev, 1)
    draft_usable = (own_reach > 0.5)[None, :, None, None, :, :]
    draft_part = partial_softmax(local_queries, tree_keys, tree_values, draft_usable, score_scale)
    source_blocks = source_x * ring + my_z
    limit = lengths[my_request] - source_blocks * block_len
    packed_out = block_attention(limit, group_rows, blocks_kv, width_q, block_len)
    head_count = width_q // HEAD_SIZE
    width_out = width_q
    moved = lax.all_to_all(
        packed_out.reshape(ring, rows_dev, -1), "bz", split_axis=0, concat_axis=0, tiled=True
    )
    spread = merge_and_spread(moved, draft_part, lax.axis_size(blk))
    every_row = lax.all_to_all(spread, blk, split_axis=0, concat_axis=0, tiled=True).reshape(
        -1, width_q
    )
    partial = jnp.dot(every_row, out_weight, preferred_element_type=jnp.float32)
    out_rows = partial.shape[0] // kv_count
    arrived = lax.all_to_all(
        partial.reshape(kv_count, out_rows, partial.shape[1]),
        "kv",
        split_axis=0,
        concat_axis=0,
        tiled=True,
    )
    projected = jnp.sum(arrived, axis=0).astype(jnp.bfloat16)
    positions_here = my_block * block_len + jnp.arange(block_len, dtype=jnp.int32)
    offset = positions_here[None, :] - lengths[:, None]
    written = (offset >= 0) & (offset < accepted_count[:, None])
    path_all = jnp.roll(path_rel[(-jnp.arange(lanes)) % lanes], my_x, axis=0)
    new_cache_keys = place_rows(path_all[..., :cache_width], offset, written, cached_key_vectors)
    new_cache_values = place_rows(
        path_all[..., cache_width:], offset, written, cached_value_vectors
    )
    return (projected, new_cache_keys, new_cache_values)


def solution(mesh):
    kv_size, blk_size = mesh.devices.shape
    requests = 4
    ring = blk_size // requests
    grid_mesh = Mesh(mesh.devices.reshape(kv_size, requests, ring), ("kv", "bx", "bz"))
    blk = ("bx", "bz")
    return jax.shard_map(
        on_device,
        mesh=grid_mesh,
        in_specs=(
            P(blk, "kv"),
            P(blk, "kv"),
            P(blk, "kv"),
            P(None, blk, "kv"),
            P(None, blk, "kv"),
            P("kv", blk),
            P(),
            P(),
            P(),
            P(),
        ),
        out_specs=(P("kv", blk), P(None, blk, "kv"), P(None, blk, "kv")),
        check_vma=False,
    )
```

```python
import functools
import math

import jax
import jax.numpy as jnp
from jax import lax
from jax.sharding import Mesh, PartitionSpec as P
from jax.experimental import pallas as pl
from jax.experimental.pallas import tpu as pltpu

HEAD_SIZE = 128
TREE_TOKENS = 64
ACC = 8


NEG_FLOOR = -1e30


def ancestors(parent_rows):
    node_ids = jnp.arange(TREE_TOKENS, dtype=jnp.int32)
    parent_link = (
        (parent_rows[:, :, None] == node_ids[None, None, :]) & (node_ids[None, :, None] >= 1)
    ).astype(jnp.float32)
    reachable = jnp.eye(TREE_TOKENS, dtype=jnp.float32)[None] + parent_link
    for doubling in range((TREE_TOKENS - 1).bit_length()):
        reachable = jnp.minimum(
            reachable
            + jnp.einsum("rij,rjk->rik", reachable, reachable, precision=lax.Precision.HIGHEST),
            1.0,
        )
    return reachable


def partial_softmax(query_vectors, key_rows, value_rows, usable, score_scale):
    scores = (
        jnp.einsum(
            "rtkgh,rbpkh->brkgtp", query_vectors, key_rows, preferred_element_type=jnp.float32
        )
        * score_scale
    )
    scores = jnp.where(usable, scores, NEG_FLOOR)
    peak_score = jnp.max(scores, axis=-1)
    weights = jnp.where(usable, jnp.exp(scores - peak_score[..., None]), 0.0)
    weight_sum = jnp.sum(weights, axis=-1)
    weighted = jnp.einsum(
        "brkgtp,rbpkh->brtkgh",
        weights.astype(jnp.bfloat16),
        value_rows,
        preferred_element_type=jnp.float32,
    )
    block_count, req_count, kv_count, query_group_width, row_count = peak_score.shape
    weighted = weighted.reshape(
        block_count, req_count * row_count, kv_count * query_group_width * value_rows.shape[-1]
    )
    peak_score = peak_score.transpose(0, 1, 4, 2, 3).reshape(
        block_count, req_count * row_count, kv_count * query_group_width
    )
    weight_sum = weight_sum.transpose(0, 1, 4, 2, 3).reshape(
        block_count, req_count * row_count, kv_count * query_group_width
    )
    return (weighted, peak_score, weight_sum)


def merge_parts(cache_part, draft_part, head_dim):
    cache_out, cache_peak, cache_sum = cache_part
    draft_out, draft_peak, draft_sum = draft_part
    cache_out = cache_out.astype(jnp.float32)
    overall = jnp.maximum(jnp.max(cache_peak, axis=0), draft_peak[0])
    cache_factor = jnp.exp(cache_peak - overall[None])
    draft_factor = jnp.exp(draft_peak[0] - overall)
    denominator = jnp.sum(cache_factor * cache_sum, axis=0) + draft_factor * draft_sum[0]
    block_count, row_count, head_count = cache_peak.shape
    numerator = jnp.sum(
        cache_factor[..., None] * cache_out.reshape(block_count, row_count, head_count, head_dim),
        axis=0,
    )
    numerator = numerator + draft_factor[..., None] * draft_out[0].reshape(
        row_count, head_count, head_dim
    )
    return (
        (numerator / denominator[..., None])
        .reshape(row_count, head_count * head_dim)
        .astype(jnp.bfloat16)
    )


def place_rows(sources, slot_index, written, cache_rows):
    slot_ids = jnp.arange(sources.shape[1], dtype=jnp.int32)
    selector = ((slot_index[:, :, None] == slot_ids[None, None, :]) & written[:, :, None]).astype(
        jnp.bfloat16
    )
    placed = jnp.einsum(
        "rps,rsc->rpc", selector, sources, preferred_element_type=jnp.float32
    ).astype(jnp.bfloat16)
    return jnp.where(written[:, :, None], placed, cache_rows)


def split_three(x):
    hi = x.astype(jnp.bfloat16)
    rest = x - hi.astype(jnp.float32)
    mid = rest.astype(jnp.bfloat16)
    lo = (rest - mid.astype(jnp.float32)).astype(jnp.bfloat16)
    return hi, mid, lo


def block_attention_kernel(block_len, limit_ref, q_ref, *refs):
    kv_refs, (out_ref, stats_ref) = refs[:-2], refs[-2:]
    blocks = len(kv_refs)
    rows = out_ref.shape[0]
    heads = stats_ref.shape[1] // 2
    score_scale = 1.0 / math.sqrt(HEAD_SIZE)
    q = jnp.concatenate(
        [q_ref[:, h * HEAD_SIZE : (h + 1) * HEAD_SIZE] for h in range(heads)], axis=0
    )
    scores = []
    valids = []
    for b in range(blocks):
        s = (
            lax.dot_general(
                q,
                kv_refs[b][:block_len, :HEAD_SIZE],
                (((1,), (1,)), ((), ())),
                preferred_element_type=jnp.float32,
            )
            * score_scale
        )
        valid = lax.broadcasted_iota(jnp.int32, s.shape, 1) < limit_ref[b]
        scores.append(jnp.where(valid, s, NEG_FLOOR))
        valids.append(valid)
    peak = jnp.max(scores[0], axis=1, keepdims=True)
    for s in scores[1:]:
        peak = jnp.maximum(peak, jnp.max(s, axis=1, keepdims=True))
    total = jnp.zeros_like(peak)
    out = jnp.zeros((q.shape[0], HEAD_SIZE), jnp.float32)
    for b in range(blocks):
        weights = jnp.where(valids[b], jnp.exp(scores[b] - peak), 0.0)
        total = total + jnp.sum(weights, axis=1, keepdims=True)
        out = out + jnp.dot(
            weights.astype(jnp.bfloat16),
            kv_refs[b][:block_len, HEAD_SIZE:],
            preferred_element_type=jnp.float32,
        )
    out = out.astype(out_ref.dtype)
    for h in range(heads):
        here = slice(h * rows, (h + 1) * rows)
        out_ref[:, h * HEAD_SIZE : (h + 1) * HEAD_SIZE] = out[here]
        stats_ref[:, h : h + 1] = peak[here]
        stats_ref[:, heads + h : heads + h + 1] = total[here]
    width = heads * HEAD_SIZE
    stats = stats_ref[...]
    for j, part in enumerate(split_three(stats)):
        out_ref[:, width + j * 2 * heads : width + (j + 1) * 2 * heads] = part


def block_attention(limit, group_rows, blocks_kv, width, block_len):
    rows = group_rows.shape[0]
    heads = width // HEAD_SIZE
    blocks = len(blocks_kv)
    vmem = pl.BlockSpec(memory_space=pltpu.VMEM)
    return pl.pallas_call(
        functools.partial(block_attention_kernel, block_len),
        out_shape=jax.ShapeDtypeStruct((rows, width + 6 * heads), jnp.bfloat16),
        in_specs=[pl.BlockSpec(memory_space=pltpu.SMEM), vmem] + [vmem] * blocks,
        out_specs=vmem,
        scratch_shapes=[pltpu.VMEM((rows, 2 * heads), jnp.float32)],
        cost_estimate=pl.CostEstimate(
            flops=4 * rows * heads * blocks * block_len * HEAD_SIZE,
            transcendentals=rows * heads * blocks * block_len,
            bytes_accessed=2 * (rows * width + 2 * blocks * block_len * HEAD_SIZE + rows * (width + 6 * heads)),
        ),
    )(limit, group_rows, *blocks_kv)


def shifted(block, axis_name, shift):
    count = lax.axis_size(axis_name)
    return lax.ppermute(block, axis_name, [(i, (i + shift) % count) for i in range(count)])


def gather_rows(block, axis_name):
    count = lax.axis_size(axis_name)
    spread = jnp.broadcast_to(block[None], (count,) + block.shape)
    moved = lax.all_to_all(spread, axis_name, split_axis=0, concat_axis=0, tiled=True)
    return moved.reshape((count * block.shape[0],) + block.shape[1:])


def on_device(
    queries,
    draft_token_keys,
    draft_token_values,
    cached_key_vectors,
    cached_value_vectors,
    out_weight,
    lengths,
    parents,
    accepted_nodes,
    accepted_count,
):
    blk = ("bx", "bz")
    kv_count = lax.axis_size("kv")
    ring = lax.axis_size("bz")
    my_block = lax.axis_index(blk)
    my_x = lax.axis_index("bx")
    my_z = lax.axis_index("bz")
    rows_dev, width_q = queries.shape
    requests = lengths.shape[0]
    cache_width = cached_key_vectors.shape[2]
    kv_local = cache_width // HEAD_SIZE
    query_group_width = width_q // (kv_local * HEAD_SIZE)
    block_len = cached_key_vectors.shape[1]
    score_scale = 1.0 / math.sqrt(HEAD_SIZE)
    my_request = my_x
    node_start = my_z * rows_dev
    local_queries = queries.reshape(1, rows_dev, kv_local, query_group_width, HEAD_SIZE)
    own_draft = jnp.concatenate([draft_token_keys, draft_token_values], axis=1)
    group_rows = gather_rows(jnp.concatenate([queries, own_draft], axis=1), "bz")
    cache_pair = jnp.concatenate([cached_key_vectors, cached_value_vectors], axis=2)
    path_pick = (
        accepted_nodes[my_request][:, None] == jnp.arange(TREE_TOKENS, dtype=jnp.int32)[None, :]
    ).astype(jnp.bfloat16)
    path_rows = jnp.dot(
        path_pick, group_rows[:, width_q:], preferred_element_type=jnp.float32
    ).astype(jnp.bfloat16)
    lanes = cache_pair.shape[0]
    blocks_kv = [lax.dynamic_index_in_dim(cache_pair, my_x, 0, False)] + [
        shifted(lax.dynamic_index_in_dim(cache_pair, (my_x + k) % lanes, 0, False), "bx", k)
        for k in range(1, lanes)
    ]
    path_rel = jnp.stack(
        [path_rows] + [shifted(path_rows, "bx", k) for k in range(1, lanes)], axis=0
    )
    source_x = (my_x - jnp.arange(lanes, dtype=jnp.int32)) % lanes
    tree_keys = group_rows[:, width_q : width_q + cache_width].reshape(
        1, 1, TREE_TOKENS, kv_local, HEAD_SIZE
    )
    tree_values = group_rows[:, width_q + cache_width :].reshape(
        1, 1, TREE_TOKENS, kv_local, HEAD_SIZE
    )
    reachable = ancestors(lax.dynamic_slice_in_dim(parents, my_request, 1, 0))
    own_reach = lax.dynamic_slice_in_dim(reachable, node_start, rows_dev, 1)
    draft_usable = (own_reach > 0.5)[None, :, None, None, :, :]
    draft_part = partial_softmax(local_queries, tree_keys, tree_values, draft_usable, score_scale)
    source_blocks = source_x * ring + my_z
    limit = lengths[my_request] - source_blocks * block_len
    packed_out = block_attention(limit, group_rows, blocks_kv, width_q, block_len)
    head_count = width_q // HEAD_SIZE
    width_out = width_q
    moved = lax.all_to_all(
        packed_out.reshape(ring, rows_dev, -1), "bz", split_axis=0, concat_axis=0, tiled=True
    )
    parts = [
        moved[..., width_out + j * 2 * head_count : width_out + (j + 1) * 2 * head_count].astype(
            jnp.float32
        )
        for j in range(3)
    ]
    moved_stats = (parts[0] + parts[1]) + parts[2]
    cache_part = (
        moved[..., :width_out],
        moved_stats[..., :head_count],
        moved_stats[..., head_count:],
    )
    attention = merge_parts(cache_part, draft_part, HEAD_SIZE)
    every_row = gather_rows(attention, blk)
    partial = jnp.dot(every_row, out_weight, preferred_element_type=jnp.float32)
    out_rows = partial.shape[0] // kv_count
    arrived = lax.all_to_all(
        partial.reshape(kv_count, out_rows, partial.shape[1]),
        "kv",
        split_axis=0,
        concat_axis=0,
        tiled=True,
    )
    projected = jnp.sum(arrived, axis=0).astype(jnp.bfloat16)
    positions_here = my_block * block_len + jnp.arange(block_len, dtype=jnp.int32)
    offset = positions_here[None, :] - lengths[:, None]
    written = (offset >= 0) & (offset < accepted_count[:, None])
    path_all = jnp.roll(path_rel[(-jnp.arange(lanes)) % lanes], my_x, axis=0)
    new_cache_keys = place_rows(path_all[..., :cache_width], offset, written, cached_key_vectors)
    new_cache_values = place_rows(
        path_all[..., cache_width:], offset, written, cached_value_vectors
    )
    return (projected, new_cache_keys, new_cache_values)


def solution(mesh):
    kv_size, blk_size = mesh.devices.shape
    requests = 4
    ring = blk_size // requests
    grid_mesh = Mesh(mesh.devices.reshape(kv_size, requests, ring), ("kv", "bx", "bz"))
    blk = ("bx", "bz")
    return jax.shard_map(
        on_device,
        mesh=grid_mesh,
        in_specs=(
            P(blk, "kv"),
            P(blk, "kv"),
            P(blk, "kv"),
            P(None, blk, "kv"),
            P(None, blk, "kv"),
            P("kv", blk),
            P(),
            P(),
            P(),
            P(),
        ),
        out_specs=(P("kv", blk), P(None, blk, "kv"), P(None, blk, "kv")),
        check_vma=False,
    )
```

```python
import functools
import math

import jax
import jax.numpy as jnp
from jax import lax
from jax.sharding import Mesh, PartitionSpec as P
from jax.experimental import pallas as pl
from jax.experimental.pallas import tpu as pltpu

HEAD_SIZE = 128
TREE_TOKENS = 64


NEG_FLOOR = -1e30


def ancestors(parent_rows):
    node_ids = jnp.arange(TREE_TOKENS, dtype=jnp.int32)
    parent_link = (
        (parent_rows[:, :, None] == node_ids[None, None, :]) & (node_ids[None, :, None] >= 1)
    ).astype(jnp.float32)
    reachable = jnp.eye(TREE_TOKENS, dtype=jnp.float32)[None] + parent_link
    for _ in range((TREE_TOKENS - 1).bit_length()):
        reachable = jnp.minimum(
            reachable
            + jnp.einsum("rij,rjk->rik", reachable, reachable, precision=lax.Precision.HIGHEST),
            1.0,
        )
    return reachable


def partial_softmax(query_vectors, key_rows, value_rows, usable, score_scale):
    scores = (
        jnp.einsum(
            "rtkgh,rbpkh->brkgtp", query_vectors, key_rows, preferred_element_type=jnp.float32
        )
        * score_scale
    )
    scores = jnp.where(usable, scores, NEG_FLOOR)
    peak_score = jnp.max(scores, axis=-1)
    weights = jnp.where(usable, jnp.exp(scores - peak_score[..., None]), 0.0)
    weight_sum = jnp.sum(weights, axis=-1)
    weighted = jnp.einsum(
        "brkgtp,rbpkh->brtkgh",
        weights.astype(jnp.bfloat16),
        value_rows,
        preferred_element_type=jnp.float32,
    )
    block_count, req_count, kv_count, query_group_width, row_count = peak_score.shape
    weighted = weighted.reshape(
        block_count, req_count * row_count, kv_count * query_group_width * value_rows.shape[-1]
    )
    peak_score = peak_score.transpose(0, 1, 4, 2, 3).reshape(
        block_count, req_count * row_count, kv_count * query_group_width
    )
    weight_sum = weight_sum.transpose(0, 1, 4, 2, 3).reshape(
        block_count, req_count * row_count, kv_count * query_group_width
    )
    return (weighted, peak_score, weight_sum)


def merge_parts(cache_part, draft_part, head_dim):
    cache_out, cache_peak, cache_sum = cache_part
    draft_out, draft_peak, draft_sum = draft_part
    cache_out = cache_out.astype(jnp.float32)
    overall = jnp.maximum(jnp.max(cache_peak, axis=0), draft_peak[0])
    cache_factor = jnp.exp(cache_peak - overall[None])
    draft_factor = jnp.exp(draft_peak[0] - overall)
    denominator = jnp.sum(cache_factor * cache_sum, axis=0) + draft_factor * draft_sum[0]
    block_count, row_count, head_count = cache_peak.shape
    numerator = jnp.sum(
        cache_factor[..., None] * cache_out.reshape(block_count, row_count, head_count, head_dim),
        axis=0,
    )
    numerator = numerator + draft_factor[..., None] * draft_out[0].reshape(
        row_count, head_count, head_dim
    )
    return (
        (numerator / denominator[..., None])
        .reshape(row_count, head_count * head_dim)
        .astype(jnp.bfloat16)
    )


def place_rows(sources, slot_index, written, cache_rows):
    slot_ids = jnp.arange(sources.shape[1], dtype=jnp.int32)
    selector = ((slot_index[:, :, None] == slot_ids[None, None, :]) & written[:, :, None]).astype(
        jnp.bfloat16
    )
    placed = jnp.einsum(
        "rps,rsc->rpc", selector, sources, preferred_element_type=jnp.float32
    ).astype(jnp.bfloat16)
    return jnp.where(written[:, :, None], placed, cache_rows)


def split_three(x):
    hi = x.astype(jnp.bfloat16)
    rest = x - hi.astype(jnp.float32)
    mid = rest.astype(jnp.bfloat16)
    lo = (rest - mid.astype(jnp.float32)).astype(jnp.bfloat16)
    return hi, mid, lo


def block_attention_kernel(block_len, limit_ref, q_ref, *refs):
    kv_refs, (out_ref, stats_ref) = refs[:-2], refs[-2:]
    blocks = len(kv_refs)
    rows = out_ref.shape[0]
    heads = stats_ref.shape[1] // 2
    score_scale = 1.0 / math.sqrt(HEAD_SIZE)
    q = jnp.concatenate(
        [q_ref[:, h * HEAD_SIZE : (h + 1) * HEAD_SIZE] for h in range(heads)], axis=0
    )
    scores = []
    valids = []
    for b in range(blocks):
        s = (
            lax.dot_general(
                q,
                kv_refs[b][:block_len, :HEAD_SIZE],
                (((1,), (1,)), ((), ())),
                preferred_element_type=jnp.float32,
            )
            * score_scale
        )
        valid = lax.broadcasted_iota(jnp.int32, s.shape, 1) < limit_ref[b]
        scores.append(jnp.where(valid, s, NEG_FLOOR))
        valids.append(valid)
    peak = jnp.max(scores[0], axis=1, keepdims=True)
    for s in scores[1:]:
        peak = jnp.maximum(peak, jnp.max(s, axis=1, keepdims=True))
    total = jnp.zeros_like(peak)
    out = jnp.zeros((q.shape[0], HEAD_SIZE), jnp.float32)
    for b in range(blocks):
        weights = jnp.where(valids[b], jnp.exp(scores[b] - peak), 0.0)
        total = total + jnp.sum(weights, axis=1, keepdims=True)
        out = out + jnp.dot(
            weights.astype(jnp.bfloat16),
            kv_refs[b][:block_len, HEAD_SIZE:],
            preferred_element_type=jnp.float32,
        )
    out = out.astype(out_ref.dtype)
    for h in range(heads):
        here = slice(h * rows, (h + 1) * rows)
        out_ref[:, h * HEAD_SIZE : (h + 1) * HEAD_SIZE] = out[here]
        stats_ref[:, h : h + 1] = peak[here]
        stats_ref[:, heads + h : heads + h + 1] = total[here]
    width = heads * HEAD_SIZE
    stats = stats_ref[...]
    for j, part in enumerate(split_three(stats)):
        out_ref[:, width + j * 2 * heads : width + (j + 1) * 2 * heads] = part


def block_attention(limit, group_rows, blocks_kv, width, block_len):
    rows = group_rows.shape[0]
    heads = width // HEAD_SIZE
    blocks = len(blocks_kv)
    vmem = pl.BlockSpec(memory_space=pltpu.VMEM)
    return pl.pallas_call(
        functools.partial(block_attention_kernel, block_len),
        out_shape=jax.ShapeDtypeStruct((rows, width + 6 * heads), jnp.bfloat16),
        in_specs=[pl.BlockSpec(memory_space=pltpu.SMEM), vmem] + [vmem] * blocks,
        out_specs=vmem,
        scratch_shapes=[pltpu.VMEM((rows, 2 * heads), jnp.float32)],
        cost_estimate=pl.CostEstimate(
            flops=4 * rows * heads * blocks * block_len * HEAD_SIZE,
            transcendentals=rows * heads * blocks * block_len,
            bytes_accessed=2 * (rows * width + 2 * blocks * block_len * HEAD_SIZE + rows * (width + 6 * heads)),
        ),
    )(limit, group_rows, *blocks_kv)


def shifted(block, axis_name, shift):
    count = lax.axis_size(axis_name)
    return lax.ppermute(block, axis_name, [(i, (i + shift) % count) for i in range(count)])


def gather_rows(block, axis_name):
    count = lax.axis_size(axis_name)
    spread = jnp.broadcast_to(block[None], (count,) + block.shape)
    moved = lax.all_to_all(spread, axis_name, split_axis=0, concat_axis=0, tiled=True)
    return moved.reshape((count * block.shape[0],) + block.shape[1:])


def on_device_body(
    queries,
    draft_token_keys,
    draft_token_values,
    cached_key_vectors,
    cached_value_vectors,
    out_weight,
    lengths,
    parents,
    accepted_nodes,
    accepted_count,
):
    blk = ("bx", "bz")
    kv_count = lax.axis_size("kv")
    ring = lax.axis_size("bz")
    my_block = lax.axis_index(blk)
    my_x = lax.axis_index("bx")
    my_z = lax.axis_index("bz")
    rows_dev, width_q = queries.shape
    cache_width = cached_key_vectors.shape[2]
    kv_local = cache_width // HEAD_SIZE
    query_group_width = width_q // (kv_local * HEAD_SIZE)
    block_len = cached_key_vectors.shape[1]
    score_scale = 1.0 / math.sqrt(HEAD_SIZE)
    my_request = my_x
    node_start = my_z * rows_dev
    local_queries = queries.reshape(1, rows_dev, kv_local, query_group_width, HEAD_SIZE)
    own_draft = jnp.concatenate([draft_token_keys, draft_token_values], axis=1)
    group_rows = gather_rows(jnp.concatenate([queries, own_draft], axis=1), "bz")
    cache_pair = jnp.concatenate([cached_key_vectors, cached_value_vectors], axis=2)
    path_pick = (
        accepted_nodes[my_request][:, None] == jnp.arange(TREE_TOKENS, dtype=jnp.int32)[None, :]
    ).astype(jnp.bfloat16)
    path_rows = jnp.dot(
        path_pick, group_rows[:, width_q:], preferred_element_type=jnp.float32
    ).astype(jnp.bfloat16)
    lanes = cache_pair.shape[0]
    ahead = jnp.roll(cache_pair, -my_x, axis=0)
    blocks_kv = [ahead[0]] + [shifted(ahead[k], "bx", k) for k in range(1, lanes)]
    path_rel = jnp.stack(
        [path_rows] + [shifted(path_rows, "bx", k) for k in range(1, lanes)], axis=0
    )
    source_x = (my_x - jnp.arange(lanes, dtype=jnp.int32)) % lanes
    tree_keys = group_rows[:, width_q : width_q + cache_width].reshape(
        1, 1, TREE_TOKENS, kv_local, HEAD_SIZE
    )
    tree_values = group_rows[:, width_q + cache_width :].reshape(
        1, 1, TREE_TOKENS, kv_local, HEAD_SIZE
    )
    reachable = ancestors(lax.dynamic_slice_in_dim(parents, my_request, 1, 0))
    own_reach = lax.dynamic_slice_in_dim(reachable, node_start, rows_dev, 1)
    draft_usable = (own_reach > 0.5)[None, :, None, None, :, :]
    draft_part = partial_softmax(local_queries, tree_keys, tree_values, draft_usable, score_scale)
    source_blocks = source_x * ring + my_z
    limit = lengths[my_request] - source_blocks * block_len
    packed_out = block_attention(limit, group_rows, blocks_kv, width_q, block_len)
    head_count = width_q // HEAD_SIZE
    width_out = width_q
    moved = lax.all_to_all(
        packed_out.reshape(ring, rows_dev, -1), "bz", split_axis=0, concat_axis=0, tiled=True
    )
    parts = [
        moved[..., width_out + j * 2 * head_count : width_out + (j + 1) * 2 * head_count].astype(
            jnp.float32
        )
        for j in range(3)
    ]
    moved_stats = (parts[0] + parts[1]) + parts[2]
    cache_part = (
        moved[..., :width_out],
        moved_stats[..., :head_count],
        moved_stats[..., head_count:],
    )
    attention = merge_parts(cache_part, draft_part, HEAD_SIZE)
    every_row = gather_rows(attention, blk)
    partial = jnp.dot(every_row, out_weight, preferred_element_type=jnp.float32)
    out_rows = partial.shape[0] // kv_count
    arrived = lax.all_to_all(
        partial.reshape(kv_count, out_rows, partial.shape[1]),
        "kv",
        split_axis=0,
        concat_axis=0,
        tiled=True,
    )
    projected = jnp.sum(arrived, axis=0).astype(jnp.bfloat16)
    positions_here = my_block * block_len + jnp.arange(block_len, dtype=jnp.int32)
    offset = positions_here[None, :] - lengths[:, None]
    written = (offset >= 0) & (offset < accepted_count[:, None])
    path_all = jnp.roll(path_rel[(-jnp.arange(lanes)) % lanes], my_x, axis=0)
    new_cache_keys = place_rows(path_all[..., :cache_width], offset, written, cached_key_vectors)
    new_cache_values = place_rows(
        path_all[..., cache_width:], offset, written, cached_value_vectors
    )
    return (projected, new_cache_keys, new_cache_values)


def solution(mesh):
    kv_size, blk_size = mesh.devices.shape
    requests = 4
    ring = blk_size // requests
    grid_mesh = Mesh(mesh.devices.reshape(kv_size, requests, ring), ("kv", "bx", "bz"))
    blk = ("bx", "bz")
    return jax.shard_map(
        on_device_body,
        mesh=grid_mesh,
        in_specs=(
            P(blk, "kv"),
            P(blk, "kv"),
            P(blk, "kv"),
            P(None, blk, "kv"),
            P(None, blk, "kv"),
            P("kv", blk),
            P(),
            P(),
            P(),
            P(),
        ),
        out_specs=(P("kv", blk), P(None, blk, "kv"), P(None, blk, "kv")),
        check_vma=False,
    )
```

```python
import functools
import math

import jax
import jax.numpy as jnp
from jax import lax
from jax.sharding import Mesh, PartitionSpec as P
from jax.experimental import pallas as pl
from jax.experimental.pallas import tpu as pltpu

HEAD_SIZE = 128
TREE_TOKENS = 64


NEG_FLOOR = -1e30


def ancestors(parent_rows):
    node_ids = jnp.arange(TREE_TOKENS, dtype=jnp.int32)
    parent_link = (
        (parent_rows[:, :, None] == node_ids[None, None, :]) & (node_ids[None, :, None] >= 1)
    ).astype(jnp.float32)
    reachable = jnp.eye(TREE_TOKENS, dtype=jnp.float32)[None] + parent_link
    for _ in range((TREE_TOKENS - 1).bit_length()):
        reachable = jnp.minimum(
            reachable
            + jnp.einsum("rij,rjk->rik", reachable, reachable, precision=lax.Precision.HIGHEST),
            1.0,
        )
    return reachable


def partial_softmax(query_vectors, key_rows, value_rows, usable, score_scale):
    scores = (
        jnp.einsum(
            "rtkgh,rbpkh->brkgtp", query_vectors, key_rows, preferred_element_type=jnp.float32
        )
        * score_scale
    )
    scores = jnp.where(usable, scores, NEG_FLOOR)
    peak_score = jnp.max(scores, axis=-1)
    weights = jnp.where(usable, jnp.exp(scores - peak_score[..., None]), 0.0)
    weight_sum = jnp.sum(weights, axis=-1)
    weighted = jnp.einsum(
        "brkgtp,rbpkh->brtkgh",
        weights.astype(jnp.bfloat16),
        value_rows,
        preferred_element_type=jnp.float32,
    )
    block_count, req_count, kv_count, query_group_width, row_count = peak_score.shape
    weighted = weighted.reshape(
        block_count, req_count * row_count, kv_count * query_group_width * value_rows.shape[-1]
    )
    peak_score = peak_score.transpose(0, 1, 4, 2, 3).reshape(
        block_count, req_count * row_count, kv_count * query_group_width
    )
    weight_sum = weight_sum.transpose(0, 1, 4, 2, 3).reshape(
        block_count, req_count * row_count, kv_count * query_group_width
    )
    return (weighted, peak_score, weight_sum)


def merge_parts(cache_part, draft_part, head_dim):
    cache_out, cache_peak, cache_sum = cache_part
    draft_out, draft_peak, draft_sum = draft_part
    cache_out = cache_out.astype(jnp.float32)
    overall = jnp.maximum(jnp.max(cache_peak, axis=0), draft_peak[0])
    cache_factor = jnp.exp(cache_peak - overall[None])
    draft_factor = jnp.exp(draft_peak[0] - overall)
    denominator = jnp.sum(cache_factor * cache_sum, axis=0) + draft_factor * draft_sum[0]
    block_count, row_count, head_count = cache_peak.shape
    numerator = jnp.sum(
        cache_factor[..., None] * cache_out.reshape(block_count, row_count, head_count, head_dim),
        axis=0,
    )
    numerator = numerator + draft_factor[..., None] * draft_out[0].reshape(
        row_count, head_count, head_dim
    )
    return (
        (numerator / denominator[..., None])
        .reshape(row_count, head_count * head_dim)
        .astype(jnp.bfloat16)
    )


def place_rows(sources, slot_index, written, cache_rows):
    slot_ids = jnp.arange(sources.shape[1], dtype=jnp.int32)
    selector = ((slot_index[:, :, None] == slot_ids[None, None, :]) & written[:, :, None]).astype(
        jnp.bfloat16
    )
    placed = jnp.einsum(
        "rps,rsc->rpc", selector, sources, preferred_element_type=jnp.float32
    ).astype(jnp.bfloat16)
    return jnp.where(written[:, :, None], placed, cache_rows)


def split_three(x):
    hi = x.astype(jnp.bfloat16)
    rest = x - hi.astype(jnp.float32)
    mid = rest.astype(jnp.bfloat16)
    lo = (rest - mid.astype(jnp.float32)).astype(jnp.bfloat16)
    return hi, mid, lo


def block_attention_kernel(block_len, ring, meta_ref, q_ref, *refs):
    kv_refs, (out_ref, stats_ref) = refs[:-2], refs[-2:]
    blocks = len(kv_refs)
    requests = meta_ref.shape[0] - 2
    my_x = meta_ref[requests]
    my_z = meta_ref[requests + 1]
    length = meta_ref[my_x]
    rows = out_ref.shape[0]
    heads = stats_ref.shape[1] // 2
    score_scale = 1.0 / math.sqrt(HEAD_SIZE)
    q = jnp.concatenate(
        [q_ref[:, h * HEAD_SIZE : (h + 1) * HEAD_SIZE] for h in range(heads)], axis=0
    )
    scores = []
    valids = []
    for b in range(blocks):
        s = (
            lax.dot_general(
                q,
                kv_refs[b][:block_len, :HEAD_SIZE],
                (((1,), (1,)), ((), ())),
                preferred_element_type=jnp.float32,
            )
            * score_scale
        )
        source_x = (my_x - b + blocks) % blocks
        limit = length - (source_x * ring + my_z) * block_len
        valid = lax.broadcasted_iota(jnp.int32, s.shape, 1) < limit
        scores.append(jnp.where(valid, s, NEG_FLOOR))
        valids.append(valid)
    peak = jnp.max(scores[0], axis=1, keepdims=True)
    for s in scores[1:]:
        peak = jnp.maximum(peak, jnp.max(s, axis=1, keepdims=True))
    total = jnp.zeros_like(peak)
    out = jnp.zeros((q.shape[0], HEAD_SIZE), jnp.float32)
    for b in range(blocks):
        weights = jnp.where(valids[b], jnp.exp(scores[b] - peak), 0.0)
        total = total + jnp.sum(weights, axis=1, keepdims=True)
        out = out + jnp.dot(
            weights.astype(jnp.bfloat16),
            kv_refs[b][:block_len, HEAD_SIZE:],
            preferred_element_type=jnp.float32,
        )
    out = out.astype(out_ref.dtype)
    for h in range(heads):
        here = slice(h * rows, (h + 1) * rows)
        out_ref[:, h * HEAD_SIZE : (h + 1) * HEAD_SIZE] = out[here]
        stats_ref[:, h : h + 1] = peak[here]
        stats_ref[:, heads + h : heads + h + 1] = total[here]
    width = heads * HEAD_SIZE
    stats = stats_ref[...]
    for j, part in enumerate(split_three(stats)):
        out_ref[:, width + j * 2 * heads : width + (j + 1) * 2 * heads] = part


def block_attention(meta, group_rows, blocks_kv, width, block_len, ring):
    rows = group_rows.shape[0]
    heads = width // HEAD_SIZE
    blocks = len(blocks_kv)
    vmem = pl.BlockSpec(memory_space=pltpu.VMEM)
    return pl.pallas_call(
        functools.partial(block_attention_kernel, block_len, ring),
        out_shape=jax.ShapeDtypeStruct((rows, width + 6 * heads), jnp.bfloat16),
        in_specs=[pl.BlockSpec(memory_space=pltpu.SMEM), vmem] + [vmem] * blocks,
        out_specs=vmem,
        scratch_shapes=[pltpu.VMEM((rows, 2 * heads), jnp.float32)],
        cost_estimate=pl.CostEstimate(
            flops=4 * rows * heads * blocks * block_len * HEAD_SIZE,
            transcendentals=rows * heads * blocks * block_len,
            bytes_accessed=2 * (rows * width + 2 * blocks * block_len * HEAD_SIZE + rows * (width + 6 * heads)),
        ),
    )(meta, group_rows, *blocks_kv)


def shifted(block, axis_name, shift):
    count = lax.axis_size(axis_name)
    return lax.ppermute(block, axis_name, [(i, (i + shift) % count) for i in range(count)])


def gather_rows(block, axis_name):
    count = lax.axis_size(axis_name)
    spread = jnp.broadcast_to(block[None], (count,) + block.shape)
    moved = lax.all_to_all(spread, axis_name, split_axis=0, concat_axis=0, tiled=True)
    return moved.reshape((count * block.shape[0],) + block.shape[1:])


def on_device_body(
    queries,
    draft_token_keys,
    draft_token_values,
    cached_key_vectors,
    cached_value_vectors,
    out_weight,
    lengths,
    parents,
    accepted_nodes,
    accepted_count,
):
    blk = ("bx", "bz")
    kv_count = lax.axis_size("kv")
    ring = lax.axis_size("bz")
    my_block = lax.axis_index(blk)
    my_x = lax.axis_index("bx")
    my_z = lax.axis_index("bz")
    rows_dev, width_q = queries.shape
    cache_width = cached_key_vectors.shape[2]
    kv_local = cache_width // HEAD_SIZE
    query_group_width = width_q // (kv_local * HEAD_SIZE)
    block_len = cached_key_vectors.shape[1]
    score_scale = 1.0 / math.sqrt(HEAD_SIZE)
    my_request = my_x
    node_start = my_z * rows_dev
    local_queries = queries.reshape(1, rows_dev, kv_local, query_group_width, HEAD_SIZE)
    own_draft = jnp.concatenate([draft_token_keys, draft_token_values], axis=1)
    group_rows = gather_rows(jnp.concatenate([queries, own_draft], axis=1), "bz")
    cache_pair = jnp.concatenate([cached_key_vectors, cached_value_vectors], axis=2)
    path_pick = (
        accepted_nodes[my_request][:, None] == jnp.arange(TREE_TOKENS, dtype=jnp.int32)[None, :]
    ).astype(jnp.bfloat16)
    path_rows = jnp.dot(
        path_pick, group_rows[:, width_q:], preferred_element_type=jnp.float32
    ).astype(jnp.bfloat16)
    lanes = cache_pair.shape[0]
    ahead = jnp.roll(cache_pair, -my_x, axis=0)
    blocks_kv = [ahead[0]] + [shifted(ahead[k], "bx", k) for k in range(1, lanes)]
    path_rel = jnp.stack(
        [path_rows] + [shifted(path_rows, "bx", k) for k in range(1, lanes)], axis=0
    )
    source_x = (my_x - jnp.arange(lanes, dtype=jnp.int32)) % lanes
    tree_keys = group_rows[:, width_q : width_q + cache_width].reshape(
        1, 1, TREE_TOKENS, kv_local, HEAD_SIZE
    )
    tree_values = group_rows[:, width_q + cache_width :].reshape(
        1, 1, TREE_TOKENS, kv_local, HEAD_SIZE
    )
    reachable = ancestors(lax.dynamic_slice_in_dim(parents, my_request, 1, 0))
    own_reach = lax.dynamic_slice_in_dim(reachable, node_start, rows_dev, 1)
    draft_usable = (own_reach > 0.5)[None, :, None, None, :, :]
    draft_part = partial_softmax(local_queries, tree_keys, tree_values, draft_usable, score_scale)
    meta = jnp.concatenate([lengths, jnp.stack([my_x, my_z]).astype(jnp.int32)])
    packed_out = block_attention(meta, group_rows, blocks_kv, width_q, block_len, ring)
    head_count = width_q // HEAD_SIZE
    width_out = width_q
    moved = lax.all_to_all(
        packed_out.reshape(ring, rows_dev, -1), "bz", split_axis=0, concat_axis=0, tiled=True
    )
    parts = [
        moved[..., width_out + j * 2 * head_count : width_out + (j + 1) * 2 * head_count].astype(
            jnp.float32
        )
        for j in range(3)
    ]
    moved_stats = (parts[0] + parts[1]) + parts[2]
    cache_part = (
        moved[..., :width_out],
        moved_stats[..., :head_count],
        moved_stats[..., head_count:],
    )
    attention = merge_parts(cache_part, draft_part, HEAD_SIZE)
    every_row = gather_rows(attention, blk)
    partial = jnp.dot(every_row, out_weight, preferred_element_type=jnp.float32)
    out_rows = partial.shape[0] // kv_count
    arrived = lax.all_to_all(
        partial.reshape(kv_count, out_rows, partial.shape[1]),
        "kv",
        split_axis=0,
        concat_axis=0,
        tiled=True,
    )
    projected = jnp.sum(arrived, axis=0).astype(jnp.bfloat16)
    positions_here = my_block * block_len + jnp.arange(block_len, dtype=jnp.int32)
    offset = positions_here[None, :] - lengths[:, None]
    written = (offset >= 0) & (offset < accepted_count[:, None])
    path_all = jnp.roll(path_rel[(-jnp.arange(lanes)) % lanes], my_x, axis=0)
    new_cache_keys = place_rows(path_all[..., :cache_width], offset, written, cached_key_vectors)
    new_cache_values = place_rows(
        path_all[..., cache_width:], offset, written, cached_value_vectors
    )
    return (projected, new_cache_keys, new_cache_values)


def solution(mesh):
    kv_size, blk_size = mesh.devices.shape
    requests = 4
    ring = blk_size // requests
    grid_mesh = Mesh(mesh.devices.reshape(kv_size, requests, ring), ("kv", "bx", "bz"))
    blk = ("bx", "bz")
    return jax.shard_map(
        on_device_body,
        mesh=grid_mesh,
        in_specs=(
            P(blk, "kv"),
            P(blk, "kv"),
            P(blk, "kv"),
            P(None, blk, "kv"),
            P(None, blk, "kv"),
            P("kv", blk),
            P(),
            P(),
            P(),
            P(),
        ),
        out_specs=(P("kv", blk), P(None, blk, "kv"), P(None, blk, "kv")),
        check_vma=False,
    )
```
